256 devices in a mesh: px: 32 (over z, x_hi, core), py: 8 (over y, x_lo).
Axes of the slice: x: 4 (x_hi: 2, x_lo: 2; x = x_hi * 2 + x_lo), y: 4, z: 8, core: 2. Of those that a mesh axis runs over, the one named last changes fastest.
Arguments:
- table: float32 [25, 50, 1000], replicated, may hold values from -1 to 1
- charge: float32 [128, 32, 8], P('px', 'py'), may hold values from 0.1 to 1
- hit_bins: int32 [128, 32, 8], P('px', 'py'), may hold values from 0 to 49
- hit_ticks: int32 [128, 32, 8], P('px', 'py'), may hold values from 0 to 23
- active: int32 [128, 32], P('px', 'py'), may hold values 0 or 1
- measured: bfloat16 [128, 32, 1024], P('px', 'py'), may hold values from -6 to 6
- row_module: int32 [128], replicated, may hold values from 0 to 6, as said below
- col_module: int32 [32], replicated, may hold values from 0 to 4, as said below
Outputs:
- current: bfloat16 [128, 32, 1024], P('px', 'py')
- table_grad: float32 [25, 50, 1000], P(None, None, 'py')
The draws below stay inside these ranges and needn't reach their ends.
Inputs may be any that keep to these rules, and one draw needn't show every extreme that they name: `row_module`: starts at 0 and never falls; it rises by one at 6 rows. `col_module`: starts at 0 and never falls; it rises by one at 4 columns.
All inputs are finite; a program needn't handle non-finite values. No bound on the sum of `active` on one device may be relied on, other than what follows from the above.
Results may differ from the reference program's by a relative error of at most 0.014.
Values may be sent and summed in bfloat16 or wider, within the bound.
No kernel may reach another device: no remote copies, remote signals or barrier semaphores. Data moves between devices by JAX's collectives and lax.ppermute only.
A program may use at most 128 MiB of HBM per device.

```python
import math
import jax
import jax.numpy as jnp
from jax import lax

BINS = 50
OFFS = 25
TICKS = 1000
SHIFTS = 24
HITS = 8
MOD_ROWS = 7
MOD_COLS = 5
TILE_X = 4
TILE_Y = 4
NX = 128
NY = 32
WAVE = 1024


def draw_hit_bins(key, part):
    rows = jnp.arange(NX, dtype=jnp.int32)[:, None, None] // TILE_X
    cols = jnp.arange(NY, dtype=jnp.int32)[None, :, None] // TILE_Y
    tile_id = rows * (NY // TILE_Y) + cols
    jitter = jax.random.randint(jax.random.fold_in(key, 5), (NX, NY, HITS), 0, 3, dtype=jnp.int32)
    nearby = (tile_id * 7 + jitter) % BINS
    spread = jax.random.randint(jax.random.fold_in(key, 6), (NX, NY, HITS), 0, BINS, dtype=jnp.int32)
    picker = jax.random.randint(jax.random.fold_in(key, 7), (NX, NY, HITS), 0, 2, dtype=jnp.int32)
    return jnp.where(picker == 1, nearby, spread).astype(jnp.int32)


def module_ids(key, count, pieces):
    starts = jax.random.permutation(key, count - 1)[:pieces - 1] + 1
    where_row = jnp.arange(count, dtype=jnp.int32)[:, None]
    return jnp.sum((starts[None, :] <= where_row).astype(jnp.int32), axis=1).astype(jnp.int32)


def draw_row_module(key, part):
    return module_ids(jax.random.fold_in(key, 11), NX, MOD_ROWS)


def draw_col_module(key, part):
    return module_ids(jax.random.fold_in(key, 13), NY, MOD_COLS)


def with_ends(result, own_key, smallest, top_value):
    place = [jax.random.randint(jax.random.fold_in(own_key, axis), (), 0, length) for axis, length in enumerate(result.shape)]
    main_axis = result.shape.index(max(result.shape))
    neighbour = place[:main_axis] + [(place[main_axis] + 1) % result.shape[main_axis]] + place[main_axis + 1:]
    return result.at[tuple(place)].set(smallest).at[tuple(neighbour)].set(top_value)


def block_scale(stream_key, dims, cuts, low, high):
    def one(axis_at, blocks):
        heights = jax.random.uniform(jax.random.fold_in(jax.random.fold_in(stream_key, 6), axis_at), (blocks,), jnp.float32, low / len(cuts), high / len(cuts))
        return jnp.repeat(jnp.exp(heights), dims[axis_at] // blocks).reshape((-1,) + (1,) * (len(dims) - axis_at - 1))

    gain = one(*cuts[0])
    for cut in cuts[1:]:
        gain = gain * one(*cut)
    return gain


def centred(stream_key, shape, scale, bound, cuts=(), held_as=jnp.bfloat16):
    drawn = scale * jax.random.normal(stream_key, shape, jnp.float32)
    if cuts:
        drawn = drawn * block_scale(stream_key, shape, cuts, -0.22, 0.18)
    return jnp.clip(drawn, -bound, bound).astype(held_as)


def setup_inputs(seed: int = 0) -> dict:
    keys = jax.random.split(jax.random.key(seed), 9)
    return {
        "table": centred(keys[0], (OFFS, BINS, TICKS), 0.15, 1.0, (), jnp.float32),
        "charge": jnp.clip(jnp.exp(math.log(1.0) - 2.3025851 * jax.random.uniform(keys[1], (NX, NY, HITS), jnp.float32) ** block_scale(keys[1], (NX, NY, HITS), ((0, 32), (1, 8)), -0.2, 0.2)), 0.1, 1.0),
        "hit_bins": draw_hit_bins(jax.random.fold_in(keys[8], 71), 0),
        "hit_ticks": with_ends(jax.random.randint(keys[3], (NX, NY, HITS), 0, SHIFTS), jax.random.fold_in(keys[3], 1), 0, SHIFTS - 1).astype(jnp.int32),
        "active": with_ends((jax.random.randint(keys[4], (NX, NY), 0, 4) < 3).astype(jnp.int32), jax.random.fold_in(keys[4], 1), 0, 1),
        "measured": centred(keys[5], (NX, NY, WAVE), 1.0, 6.0, ((0, 32), (1, 8))),
        "row_module": draw_row_module(jax.random.fold_in(keys[8], 71), 0),
        "col_module": draw_col_module(jax.random.fold_in(keys[8], 71), 0),
    }


def bin_charges(charge, hit_bins, hit_ticks):
    tick_hot = (hit_ticks[..., None] == jnp.arange(SHIFTS, dtype=jnp.int32)).astype(jnp.float32)
    bin_hot = (hit_bins[..., None] == jnp.arange(BINS, dtype=jnp.int32)).astype(jnp.float32)
    weighted = charge.astype(jnp.float32)[..., None] * tick_hot
    return jnp.einsum('xyks,xykb->xysb', weighted, bin_hot).astype(jnp.bfloat16)


def gather_offsets(source, rows, cols, count_x, count_y):
    pieces = []
    for row_off in range(-2, 3):
        for col_off in range(-2, 3):
            partial_value = source[2 - row_off:2 - row_off + count_x, 2 - col_off:2 - col_off + count_y]
            row_same = rows[2 - row_off:2 - row_off + count_x] == rows[2:2 + count_x]
            col_same = cols[2 - col_off:2 - col_off + count_y] == cols[2:2 + count_y]
            allowed = row_same[:, None] & col_same[None, :]
            pieces.append(jnp.where(allowed[:, :, None, None], partial_value, jnp.zeros((), partial_value.dtype)))
    return jnp.stack(pieces, 0)


def shift_sum(partial_value):
    total = jnp.zeros(partial_value.shape[:2] + (TICKS + SHIFTS,), jnp.float32)
    for offset in range(SHIFTS):
        total = total + jnp.pad(partial_value[:, :, offset, :], ((0, 0), (0, 0), (offset, SHIFTS - offset)))
    return total


def windows(resid):
    return jnp.stack([resid[:, :, offset:offset + TICKS] for offset in range(SHIFTS)], axis=2)


def reference(table, charge, hit_bins, hit_ticks, active, measured, row_module, col_module):
    binned = bin_charges(charge, hit_bins, hit_ticks)
    weights = lax.optimization_barrier(table.astype(jnp.bfloat16)).astype(jnp.float32)
    padded = jnp.pad(binned, ((2, 2), (2, 2), (0, 0), (0, 0)))
    rows_pad = jnp.pad(row_module, 2, constant_values=-1)
    cols_pad = jnp.pad(col_module, 2, constant_values=-1)

    def band(carry, index):
        start = index * TILE_X
        source = lax.dynamic_slice_in_dim(padded, start, TILE_X + 4, 0)
        rows = lax.dynamic_slice_in_dim(rows_pad, start, TILE_X + 4, 0)
        stacked = gather_offsets(source, rows, cols_pad, TILE_X, NY).astype(jnp.float32)
        partial_value = jnp.einsum('oxysb,obt->xyst', stacked, weights)
        prediction = shift_sum(partial_value)
        seen = lax.dynamic_slice_in_dim(measured, start, TILE_X, 0).astype(jnp.float32)
        reads = lax.dynamic_slice_in_dim(active, start, TILE_X, 0).astype(jnp.float32)
        resid = ((prediction - seen) * reads[..., None]).astype(jnp.bfloat16)
        contrib = jnp.einsum('oxysb,xysu->obu', stacked, windows(resid).astype(jnp.float32))
        return carry + contrib, prediction.astype(jnp.bfloat16)

    initial = jnp.zeros((OFFS, BINS, TICKS), jnp.float32)
    gradient, bands = lax.scan(band, initial, jnp.arange(NX // TILE_X, dtype=jnp.int32))
    current = bands.reshape(NX, NY, TICKS + SHIFTS)
    return current, gradient / (TILE_X * TILE_Y)
```

```python
import jax
import jax.numpy as jnp
from jax import lax
from jax.sharding import PartitionSpec as P

BINS = 50
SHIFTS = 24


def passed_along(block, axis, distance):
    devices = range(lax.axis_size(axis))
    route = [(i - distance, i) for i in devices if i - distance in devices]
    return lax.ppermute(block, axis, route)


def bin_charges(charge, hit_bins, hit_ticks):
    tick_hot = (hit_ticks[..., None] == jnp.arange(SHIFTS, dtype=jnp.int32)).astype(jnp.float32)
    bin_hot = (hit_bins[..., None] == jnp.arange(BINS, dtype=jnp.int32)).astype(jnp.float32)
    weighted = charge[..., None] * tick_hot
    return jnp.einsum("xyks,xykb->xysb", weighted, bin_hot).astype(jnp.bfloat16)


def gather_offsets(source, rows, cols, count_x, count_y):
    pieces = []
    for row_off in range(-2, 3):
        for col_off in range(-2, 3):
            partial_value = source[
                2 - row_off : 2 - row_off + count_x, 2 - col_off : 2 - col_off + count_y
            ]
            row_same = rows[2 - row_off : 2 - row_off + count_x] == rows[2 : 2 + count_x]
            col_same = cols[2 - col_off : 2 - col_off + count_y] == cols[2 : 2 + count_y]
            allowed = row_same[:, None] & col_same[None, :]
            pieces.append(
                jnp.where(
                    allowed[:, :, None, None], partial_value, jnp.zeros((), partial_value.dtype)
                )
            )
    return jnp.stack(pieces, 0)


def shift_sum(partial_value, ticks):
    total = jnp.zeros(partial_value.shape[:2] + (ticks + SHIFTS,), jnp.float32)
    for offset in range(SHIFTS):
        total = total + jnp.pad(
            partial_value[:, :, offset, :], ((0, 0), (0, 0), (offset, SHIFTS - offset))
        )
    return total


def windows(resid, ticks):
    return jnp.stack([resid[:, :, offset : offset + ticks] for offset in range(SHIFTS)], axis=2)


def residual_of(prediction, measured, active):
    return (
        (prediction - measured.astype(jnp.float32)) * active.astype(jnp.float32)[..., None]
    ).astype(jnp.bfloat16)


def on_device(table, charge, hit_bins, hit_ticks, active, measured, row_module, col_module):
    tile_x, tile_y = (charge.shape[0], charge.shape[1])
    ticks = table.shape[2]
    parts_y = lax.axis_size("py")
    share = ticks // parts_y
    span = share + SHIFTS - 1
    weights = table.astype(jnp.bfloat16)
    row_start = lax.axis_index("px") * tile_x
    col_start = lax.axis_index("py") * tile_y

    deposits = jnp.stack(
        [charge, hit_bins.astype(jnp.float32), hit_ticks.astype(jnp.float32)], axis=-1
    )
    band = lax.all_gather(deposits, "py", axis=1, tiled=True)
    above = passed_along(band[tile_x - 2 :], "px", 1)
    below = passed_along(band[:2], "px", -1)
    wide = jnp.concatenate([above, band, below], axis=0)
    binned = bin_charges(
        wide[..., 0], wide[..., 1].astype(jnp.int32), wide[..., 2].astype(jnp.int32)
    )
    source = jnp.pad(binned, ((0, 0), (2, 2), (0, 0), (0, 0)))
    width = source.shape[1] - 4
    rows_wide = lax.dynamic_slice_in_dim(
        jnp.pad(row_module, 2, constant_values=-1), row_start, tile_x + 4, 0
    )
    cols_all = jnp.pad(col_module, 2, constant_values=-1)

    own_source = lax.dynamic_slice_in_dim(source, col_start, tile_y + 4, 1)
    own_cols = lax.dynamic_slice_in_dim(cols_all, col_start, tile_y + 4, 0)
    stacked = gather_offsets(own_source, rows_wide, own_cols, tile_x, tile_y)
    partial_value = jnp.einsum(
        "oxysb,obt->xyst", stacked, weights, preferred_element_type=jnp.float32
    )
    prediction = shift_sum(partial_value, ticks)
    resid = residual_of(prediction, measured, active)

    sent = jnp.stack(
        [resid[:, :, k * share : k * share + span] for k in range(parts_y)], axis=0
    )
    got = lax.all_to_all(sent, "py", 0, 0)
    band_resid = jnp.transpose(got, (1, 0, 2, 3)).reshape(tile_x, width, span)

    stacked_band = gather_offsets(source, rows_wide, cols_all, tile_x, width)
    gradient = jnp.einsum(
        "oxysb,xysu->obu",
        stacked_band,
        windows(band_resid, share),
        preferred_element_type=jnp.float32,
    )
    summed = lax.psum(gradient, "px")
    return (prediction.astype(jnp.bfloat16), summed / 16)


def solution(mesh):
    in_specs = (
        P(),
        P("px", "py", None),
        P("px", "py", None),
        P("px", "py", None),
        P("px", "py"),
        P("px", "py", None),
        P(),
        P(),
    )
    out_specs = (P("px", "py", None), P(None, None, "py"))
    return jax.shard_map(
        on_device, mesh=mesh, in_specs=in_specs, out_specs=out_specs, check_vma=False
    )
```

```python
import jax
import jax.numpy as jnp
from jax import lax
from jax.sharding import PartitionSpec as P

BINS = 50
SHIFTS = 24


def passed_along(block, axis, distance):
    devices = range(lax.axis_size(axis))
    route = [(i - distance, i) for i in devices if i - distance in devices]
    return lax.ppermute(block, axis, route)


def tree_sum(value, axis):
    count = lax.axis_size(axis)
    me = lax.axis_index(axis)
    steps = count.bit_length() - 1
    rows = value.shape[0]
    unit = -(-rows // count)
    buf = jnp.pad(value, ((0, unit * count - rows),) + ((0, 0),) * (value.ndim - 1))
    bits = []
    for k in range(steps):
        gap = 1 << k
        bit = (me >> k) & 1
        bits.append(bit)
        half = buf.shape[0] // 2
        keep = lax.dynamic_slice_in_dim(buf, bit * half, half, 0)
        send = lax.dynamic_slice_in_dim(buf, (1 - bit) * half, half, 0)
        got = lax.ppermute(send, axis, [(p, p ^ gap) for p in range(count)])
        buf = keep + got
    for k in reversed(range(steps)):
        gap = 1 << k
        got = lax.ppermute(buf, axis, [(p, p ^ gap) for p in range(count)])
        low = jnp.where(bits[k] == 0, buf, got)
        high = jnp.where(bits[k] == 0, got, buf)
        buf = jnp.concatenate([low, high], axis=0)
    return buf[:rows]


def bin_charges(charge, hit_bins, hit_ticks):
    tick_hot = (hit_ticks[..., None] == jnp.arange(SHIFTS, dtype=jnp.int32)).astype(jnp.float32)
    bin_hot = (hit_bins[..., None] == jnp.arange(BINS, dtype=jnp.int32)).astype(jnp.float32)
    weighted = charge[..., None] * tick_hot
    return jnp.einsum("xyks,xykb->xysb", weighted, bin_hot).astype(jnp.bfloat16)


def gather_offsets(source, rows, cols, count_x, count_y):
    pieces = []
    for row_off in range(-2, 3):
        for col_off in range(-2, 3):
            partial_value = source[
                2 - row_off : 2 - row_off + count_x, 2 - col_off : 2 - col_off + count_y
            ]
            row_same = rows[2 - row_off : 2 - row_off + count_x] == rows[2 : 2 + count_x]
            col_same = cols[2 - col_off : 2 - col_off + count_y] == cols[2 : 2 + count_y]
            allowed = row_same[:, None] & col_same[None, :]
            pieces.append(
                jnp.where(
                    allowed[:, :, None, None], partial_value, jnp.zeros((), partial_value.dtype)
                )
            )
    return jnp.stack(pieces, 0)


def shift_sum(partial_value, ticks):
    total = jnp.zeros(partial_value.shape[:2] + (ticks + SHIFTS,), jnp.float32)
    for offset in range(SHIFTS):
        total = total + jnp.pad(
            partial_value[:, :, offset, :], ((0, 0), (0, 0), (offset, SHIFTS - offset))
        )
    return total


def windows(resid, ticks):
    return jnp.stack([resid[:, :, offset : offset + ticks] for offset in range(SHIFTS)], axis=2)


def residual_of(prediction, measured, active):
    return (
        (prediction - measured.astype(jnp.float32)) * active.astype(jnp.float32)[..., None]
    ).astype(jnp.bfloat16)


def on_device(table, charge, hit_bins, hit_ticks, active, measured, row_module, col_module):
    tile_x, tile_y = (charge.shape[0], charge.shape[1])
    ticks = table.shape[2]
    parts_y = lax.axis_size("py")
    share = ticks // parts_y
    span = share + SHIFTS - 1
    weights = table.astype(jnp.bfloat16)
    row_start = lax.axis_index("px") * tile_x
    col_start = lax.axis_index("py") * tile_y

    deposits = jnp.stack(
        [charge, hit_bins.astype(jnp.float32), hit_ticks.astype(jnp.float32)], axis=-1
    )
    spread = jnp.broadcast_to(deposits[None], (parts_y,) + deposits.shape)
    band = jnp.transpose(lax.all_to_all(spread, "py", 0, 0), (1, 0, 2, 3, 4))
    band = band.reshape((tile_x, parts_y * tile_y) + deposits.shape[2:])
    above = passed_along(band[tile_x - 2 :], "px", 1)
    below = passed_along(band[:2], "px", -1)
    wide = jnp.concatenate([above, band, below], axis=0)
    binned = bin_charges(
        wide[..., 0], wide[..., 1].astype(jnp.int32), wide[..., 2].astype(jnp.int32)
    )
    source = jnp.pad(binned, ((0, 0), (2, 2), (0, 0), (0, 0)))
    width = source.shape[1] - 4
    rows_wide = lax.dynamic_slice_in_dim(
        jnp.pad(row_module, 2, constant_values=-1), row_start, tile_x + 4, 0
    )
    cols_all = jnp.pad(col_module, 2, constant_values=-1)

    own_source = lax.dynamic_slice_in_dim(source, col_start, tile_y + 4, 1)
    own_cols = lax.dynamic_slice_in_dim(cols_all, col_start, tile_y + 4, 0)
    stacked = gather_offsets(own_source, rows_wide, own_cols, tile_x, tile_y)
    partial_value = jnp.einsum(
        "oxysb,obt->xyst", stacked, weights, preferred_element_type=jnp.float32
    )
    prediction = shift_sum(partial_value, ticks)
    resid = residual_of(prediction, measured, active)

    sent = jnp.stack(
        [resid[:, :, k * share : k * share + span] for k in range(parts_y)], axis=0
    )
    got = lax.all_to_all(sent, "py", 0, 0)
    band_resid = jnp.transpose(got, (1, 0, 2, 3)).reshape(tile_x, width, span)

    stacked_band = gather_offsets(source, rows_wide, cols_all, tile_x, width)
    gradient = jnp.einsum(
        "oxysb,xysu->obu",
        stacked_band,
        windows(band_resid, share),
        preferred_element_type=jnp.float32,
    )
    flat = gradient.reshape(-1, share)
    summed = tree_sum(flat, "px").reshape(gradient.shape)
    return (prediction.astype(jnp.bfloat16), summed / 16)


def solution(mesh):
    in_specs = (
        P(),
        P("px", "py", None),
        P("px", "py", None),
        P("px", "py", None),
        P("px", "py"),
        P("px", "py", None),
        P(),
        P(),
    )
    out_specs = (P("px", "py", None), P(None, None, "py"))
    return jax.shard_map(
        on_device, mesh=mesh, in_specs=in_specs, out_specs=out_specs, check_vma=False
    )
```

```python
import jax
import jax.numpy as jnp
from jax import lax
from jax.sharding import PartitionSpec as P

BINS = 50
SHIFTS = 24


def passed_along(block, axis, distance):
    devices = range(lax.axis_size(axis))
    route = [(i - distance, i) for i in devices if i - distance in devices]
    return lax.ppermute(block, axis, route)


def tree_sum(value, axis):
    count = lax.axis_size(axis)
    me = lax.axis_index(axis)
    steps = count.bit_length() - 1
    rows = value.shape[0]
    unit = -(-rows // count)
    buf = jnp.pad(value, ((0, unit * count - rows),) + ((0, 0),) * (value.ndim - 1))
    bits = []
    for k in range(steps):
        gap = 1 << k
        bit = (me >> k) & 1
        bits.append(bit)
        half = buf.shape[0] // 2
        keep = lax.dynamic_slice_in_dim(buf, bit * half, half, 0)
        send = lax.dynamic_slice_in_dim(buf, (1 - bit) * half, half, 0)
        got = lax.ppermute(send, axis, [(p, p ^ gap) for p in range(count)])
        buf = keep + got
    for k in reversed(range(steps)):
        gap = 1 << k
        got = lax.ppermute(buf, axis, [(p, p ^ gap) for p in range(count)])
        low = jnp.where(bits[k] == 0, buf, got)
        high = jnp.where(bits[k] == 0, got, buf)
        buf = jnp.concatenate([low, high], axis=0)
    return buf[:rows]


def exchange_sum(value, axis):
    count = lax.axis_size(axis)
    rows = value.shape[0]
    unit = -(-rows // count)
    buf = jnp.pad(value, ((0, unit * count - rows),) + ((0, 0),) * (value.ndim - 1))
    pieces = buf.reshape((count, unit) + value.shape[1:])
    mine = jnp.sum(lax.all_to_all(pieces, axis, 0, 0), axis=0)
    spread = jnp.broadcast_to(mine[None], pieces.shape)
    every = lax.all_to_all(spread, axis, 0, 0)
    return every.reshape(buf.shape)[:rows]


def bin_charges(charge, hit_bins, hit_ticks):
    tick_hot = (hit_ticks[..., None] == jnp.arange(SHIFTS, dtype=jnp.int32)).astype(jnp.float32)
    bin_hot = (hit_bins[..., None] == jnp.arange(BINS, dtype=jnp.int32)).astype(jnp.float32)
    weighted = charge[..., None] * tick_hot
    return jnp.einsum("xyks,xykb->xysb", weighted, bin_hot).astype(jnp.bfloat16)


def gather_offsets(source, rows, cols, count_x, count_y):
    pieces = []
    for row_off in range(-2, 3):
        for col_off in range(-2, 3):
            partial_value = source[
                2 - row_off : 2 - row_off + count_x, 2 - col_off : 2 - col_off + count_y
            ]
            row_same = rows[2 - row_off : 2 - row_off + count_x] == rows[2 : 2 + count_x]
            col_same = cols[2 - col_off : 2 - col_off + count_y] == cols[2 : 2 + count_y]
            allowed = row_same[:, None] & col_same[None, :]
            pieces.append(
                jnp.where(
                    allowed[:, :, None, None], partial_value, jnp.zeros((), partial_value.dtype)
                )
            )
    return jnp.stack(pieces, 0)


def shift_sum(partial_value, ticks):
    total = jnp.zeros(partial_value.shape[:2] + (ticks + SHIFTS,), jnp.float32)
    for offset in range(SHIFTS):
        total = total + jnp.pad(
            partial_value[:, :, offset, :], ((0, 0), (0, 0), (offset, SHIFTS - offset))
        )
    return total


def windows(resid, ticks):
    return jnp.stack([resid[:, :, offset : offset + ticks] for offset in range(SHIFTS)], axis=2)


def residual_of(prediction, measured, active):
    return (
        (prediction - measured.astype(jnp.float32)) * active.astype(jnp.float32)[..., None]
    ).astype(jnp.bfloat16)


def on_device(table, charge, hit_bins, hit_ticks, active, measured, row_module, col_module):
    tile_x, tile_y = (charge.shape[0], charge.shape[1])
    ticks = table.shape[2]
    parts_y = lax.axis_size("py")
    share = ticks // parts_y
    span = share + SHIFTS - 1
    weights = table.astype(jnp.bfloat16)
    row_start = lax.axis_index("px") * tile_x
    col_start = lax.axis_index("py") * tile_y

    deposits = jnp.stack(
        [charge, hit_bins.astype(jnp.float32), hit_ticks.astype(jnp.float32)], axis=-1
    )
    spread = jnp.broadcast_to(deposits[None], (parts_y,) + deposits.shape)
    band = jnp.transpose(lax.all_to_all(spread, "py", 0, 0), (1, 0, 2, 3, 4))
    band = band.reshape((tile_x, parts_y * tile_y) + deposits.shape[2:])
    above = passed_along(band[tile_x - 2 :], "px", 1)
    below = passed_along(band[:2], "px", -1)
    wide = jnp.concatenate([above, band, below], axis=0)
    binned = bin_charges(
        wide[..., 0], wide[..., 1].astype(jnp.int32), wide[..., 2].astype(jnp.int32)
    )
    source = jnp.pad(binned, ((0, 0), (2, 2), (0, 0), (0, 0)))
    width = source.shape[1] - 4
    rows_wide = lax.dynamic_slice_in_dim(
        jnp.pad(row_module, 2, constant_values=-1), row_start, tile_x + 4, 0
    )
    cols_all = jnp.pad(col_module, 2, constant_values=-1)

    own_source = lax.dynamic_slice_in_dim(source, col_start, tile_y + 4, 1)
    own_cols = lax.dynamic_slice_in_dim(cols_all, col_start, tile_y + 4, 0)
    stacked = gather_offsets(own_source, rows_wide, own_cols, tile_x, tile_y)
    partial_value = jnp.einsum(
        "oxysb,obt->xyst", stacked, weights, preferred_element_type=jnp.float32
    )
    prediction = shift_sum(partial_value, ticks)
    resid = residual_of(prediction, measured, active)

    sent = jnp.stack(
        [resid[:, :, k * share : k * share + span] for k in range(parts_y)], axis=0
    )
    got = lax.all_to_all(sent, "py", 0, 0)
    band_resid = jnp.transpose(got, (1, 0, 2, 3)).reshape(tile_x, width, span)

    stacked_band = gather_offsets(source, rows_wide, cols_all, tile_x, width)
    gradient = jnp.einsum(
        "oxysb,xysu->obu",
        stacked_band,
        windows(band_resid, share),
        preferred_element_type=jnp.float32,
    )
    flat = gradient.reshape(-1, share)
    summed = exchange_sum(flat, "px").reshape(gradient.shape)
    return (prediction.astype(jnp.bfloat16), summed / 16)


def solution(mesh):
    in_specs = (
        P(),
        P("px", "py", None),
        P("px", "py", None),
        P("px", "py", None),
        P("px", "py"),
        P("px", "py", None),
        P(),
        P(),
    )
    out_specs = (P("px", "py", None), P(None, None, "py"))
    return jax.shard_map(
        on_device, mesh=mesh, in_specs=in_specs, out_specs=out_specs, check_vma=False
    )
```

```python
import jax
import jax.numpy as jnp
from jax import lax
from jax.sharding import PartitionSpec as P

BINS = 50
SHIFTS = 24
PX = ("pxa", "pxc")


def px_index():
    return lax.axis_index("pxa") * 2 + lax.axis_index("pxc")


def passed_along(block, axis, distance):
    devices = range(lax.axis_size("pxa") * 2)
    route = [(i - distance, i) for i in devices if i - distance in devices]
    return lax.ppermute(block, axis, route)


def tree_sum(value, axis):
    count = lax.axis_size(axis)
    me = lax.axis_index(axis)
    steps = count.bit_length() - 1
    rows = value.shape[0]
    unit = -(-rows // count)
    buf = jnp.pad(value, ((0, unit * count - rows),) + ((0, 0),) * (value.ndim - 1))
    bits = []
    for k in range(steps):
        gap = 1 << k
        bit = (me >> k) & 1
        bits.append(bit)
        half = buf.shape[0] // 2
        keep = lax.dynamic_slice_in_dim(buf, bit * half, half, 0)
        send = lax.dynamic_slice_in_dim(buf, (1 - bit) * half, half, 0)
        got = lax.ppermute(send, axis, [(p, p ^ gap) for p in range(count)])
        buf = keep + got
    for k in reversed(range(steps)):
        gap = 1 << k
        got = lax.ppermute(buf, axis, [(p, p ^ gap) for p in range(count)])
        low = jnp.where(bits[k] == 0, buf, got)
        high = jnp.where(bits[k] == 0, got, buf)
        buf = jnp.concatenate([low, high], axis=0)
    return buf[:rows]


def exchange_sum(value, axis):
    count = lax.axis_size(axis)
    rows = value.shape[0]
    unit = -(-rows // count)
    buf = jnp.pad(value, ((0, unit * count - rows),) + ((0, 0),) * (value.ndim - 1))
    pieces = buf.reshape((count, unit) + value.shape[1:])
    mine = jnp.sum(lax.all_to_all(pieces, axis, 0, 0), axis=0)
    spread = jnp.broadcast_to(mine[None], pieces.shape)
    every = lax.all_to_all(spread, axis, 0, 0)
    return every.reshape(buf.shape)[:rows]


def chip_sum(value):
    count = lax.axis_size("pxa")
    core = lax.axis_index("pxc")
    swap = [(0, 1), (1, 0)]
    rows = value.shape[0]
    unit = -(-rows // (2 * count))
    buf = jnp.pad(value, ((0, 2 * unit * count - rows),) + ((0, 0),) * (value.ndim - 1))
    half = unit * count
    keep = lax.dynamic_slice_in_dim(buf, core * half, half, 0)
    send = lax.dynamic_slice_in_dim(buf, (1 - core) * half, half, 0)
    part = keep + lax.ppermute(send, "pxc", swap)
    pieces = part.reshape((count, unit) + value.shape[1:])
    mine = jnp.sum(lax.all_to_all(pieces, "pxa", 0, 0), axis=0).astype(jnp.bfloat16)
    spread = jnp.broadcast_to(mine[None], pieces.shape)
    ours = lax.all_to_all(spread, "pxa", 0, 0).reshape((half,) + value.shape[1:])
    theirs = lax.ppermute(ours, "pxc", swap)
    low = jnp.where(core == 0, ours, theirs)
    high = jnp.where(core == 0, theirs, ours)
    return jnp.concatenate([low, high], axis=0)[:rows].astype(jnp.float32)


def bin_charges(charge, hit_bins, hit_ticks):
    tick_hot = (hit_ticks[..., None] == jnp.arange(SHIFTS, dtype=jnp.int32)).astype(jnp.float32)
    bin_hot = (hit_bins[..., None] == jnp.arange(BINS, dtype=jnp.int32)).astype(jnp.float32)
    weighted = charge[..., None] * tick_hot
    return jnp.einsum("xyks,xykb->xysb", weighted, bin_hot).astype(jnp.bfloat16)


def gather_offsets(source, rows, cols, count_x, count_y):
    pieces = []
    for row_off in range(-2, 3):
        for col_off in range(-2, 3):
            partial_value = source[
                2 - row_off : 2 - row_off + count_x, 2 - col_off : 2 - col_off + count_y
            ]
            row_same = rows[2 - row_off : 2 - row_off + count_x] == rows[2 : 2 + count_x]
            col_same = cols[2 - col_off : 2 - col_off + count_y] == cols[2 : 2 + count_y]
            allowed = row_same[:, None] & col_same[None, :]
            pieces.append(
                jnp.where(
                    allowed[:, :, None, None], partial_value, jnp.zeros((), partial_value.dtype)
                )
            )
    return jnp.stack(pieces, 0)


def shift_sum(partial_value, ticks):
    total = jnp.zeros(partial_value.shape[:2] + (ticks + SHIFTS,), jnp.float32)
    for offset in range(SHIFTS):
        total = total + jnp.pad(
            partial_value[:, :, offset, :], ((0, 0), (0, 0), (offset, SHIFTS - offset))
        )
    return total


def windows(resid, ticks):
    return jnp.stack([resid[:, :, offset : offset + ticks] for offset in range(SHIFTS)], axis=2)


def residual_of(prediction, measured, active):
    return (
        (prediction - measured.astype(jnp.float32)) * active.astype(jnp.float32)[..., None]
    ).astype(jnp.bfloat16)


def on_device(table, charge, hit_bins, hit_ticks, active, measured, row_module, col_module):
    tile_x, tile_y = (charge.shape[0], charge.shape[1])
    ticks = table.shape[2]
    parts_y = lax.axis_size("py")
    share = ticks // parts_y
    span = share + SHIFTS - 1
    weights = table.astype(jnp.bfloat16)
    row_start = px_index() * tile_x
    col_start = lax.axis_index("py") * tile_y

    deposits = jnp.stack(
        [charge, hit_bins.astype(jnp.float32), hit_ticks.astype(jnp.float32)], axis=-1
    )
    spread = jnp.broadcast_to(deposits[None], (parts_y,) + deposits.shape)
    band = jnp.transpose(lax.all_to_all(spread, "py", 0, 0), (1, 0, 2, 3, 4))
    band = band.reshape((tile_x, parts_y * tile_y) + deposits.shape[2:])
    above = passed_along(band[tile_x - 2 :], PX, 1)
    below = passed_along(band[:2], PX, -1)
    wide = jnp.concatenate([above, band, below], axis=0)
    binned = bin_charges(
        wide[..., 0], wide[..., 1].astype(jnp.int32), wide[..., 2].astype(jnp.int32)
    )
    source = jnp.pad(binned, ((0, 0), (2, 2), (0, 0), (0, 0)))
    width = source.shape[1] - 4
    rows_wide = lax.dynamic_slice_in_dim(
        jnp.pad(row_module, 2, constant_values=-1), row_start, tile_x + 4, 0
    )
    cols_all = jnp.pad(col_module, 2, constant_values=-1)

    own_source = lax.dynamic_slice_in_dim(source, col_start, tile_y + 4, 1)
    own_cols = lax.dynamic_slice_in_dim(cols_all, col_start, tile_y + 4, 0)
    stacked = gather_offsets(own_source, rows_wide, own_cols, tile_x, tile_y)
    partial_value = jnp.einsum(
        "oxysb,obt->xyst", stacked, weights, preferred_element_type=jnp.float32
    )
    prediction = shift_sum(partial_value, ticks)
    resid = residual_of(prediction, measured, active)

    sent = jnp.stack(
        [resid[:, :, k * share : k * share + span] for k in range(parts_y)], axis=0
    )
    got = lax.all_to_all(sent, "py", 0, 0)
    band_resid = jnp.transpose(got, (1, 0, 2, 3)).reshape(tile_x, width, span)

    stacked_band = gather_offsets(source, rows_wide, cols_all, tile_x, width)
    gradient = jnp.einsum(
        "oxysb,xysu->obu",
        stacked_band,
        windows(band_resid, share),
        preferred_element_type=jnp.float32,
    )
    flat = gradient.reshape(-1, share)
    summed = chip_sum(flat).reshape(gradient.shape)
    return (prediction.astype(jnp.bfloat16), summed / 16)


def solution(mesh):
    in_specs = (
        P(),
        P("px", "py", None),
        P("px", "py", None),
        P("px", "py", None),
        P("px", "py"),
        P("px", "py", None),
        P(),
        P(),
    )
    out_specs = (P("px", "py", None), P(None, None, "py"))
    rows_of = mesh.shape["px"]
    split = jax.sharding.Mesh(
        mesh.devices.reshape((rows_of // 2, 2) + mesh.devices.shape[1:]), ("pxa", "pxc", "py")
    )
    rename = lambda spec: P(*[PX if part == "px" else part for part in spec])
    return jax.shard_map(
        on_device,
        mesh=split,
        in_specs=tuple(rename(spec) for spec in in_specs),
        out_specs=tuple(rename(spec) for spec in out_specs),
        check_vma=False,
    )
```

```python
import jax
import jax.numpy as jnp
from jax import lax
from jax.sharding import PartitionSpec as P

BINS = 50
SHIFTS = 24
PX = ("pxa", "pxc")


def px_index():
    return lax.axis_index("pxa") * 2 + lax.axis_index("pxc")


def passed_along(block, axis, distance):
    devices = range(lax.axis_size("pxa") * 2)
    route = [(i - distance, i) for i in devices if i - distance in devices]
    return lax.ppermute(block, axis, route)


def tree_sum(value, axis):
    count = lax.axis_size(axis)
    me = lax.axis_index(axis)
    steps = count.bit_length() - 1
    rows = value.shape[0]
    unit = -(-rows // count)
    buf = jnp.pad(value, ((0, unit * count - rows),) + ((0, 0),) * (value.ndim - 1))
    bits = []
    for k in range(steps):
        gap = 1 << k
        bit = (me >> k) & 1
        bits.append(bit)
        half = buf.shape[0] // 2
        keep = lax.dynamic_slice_in_dim(buf, bit * half, half, 0)
        send = lax.dynamic_slice_in_dim(buf, (1 - bit) * half, half, 0)
        got = lax.ppermute(send, axis, [(p, p ^ gap) for p in range(count)])
        buf = keep + got
    for k in reversed(range(steps)):
        gap = 1 << k
        got = lax.ppermute(buf, axis, [(p, p ^ gap) for p in range(count)])
        low = jnp.where(bits[k] == 0, buf, got)
        high = jnp.where(bits[k] == 0, got, buf)
        buf = jnp.concatenate([low, high], axis=0)
    return buf[:rows]


def exchange_sum(value, axis):
    count = lax.axis_size(axis)
    rows = value.shape[0]
    unit = -(-rows // count)
    buf = jnp.pad(value, ((0, unit * count - rows),) + ((0, 0),) * (value.ndim - 1))
    pieces = buf.reshape((count, unit) + value.shape[1:])
    mine = jnp.sum(lax.all_to_all(pieces, axis, 0, 0), axis=0)
    spread = jnp.broadcast_to(mine[None], pieces.shape)
    every = lax.all_to_all(spread, axis, 0, 0)
    return every.reshape(buf.shape)[:rows]


def chip_sum(value):
    count = lax.axis_size("pxa")
    core = lax.axis_index("pxc")
    swap = [(0, 1), (1, 0)]
    rows = value.shape[0]
    unit = -(-rows // (2 * count))
    buf = jnp.pad(value, ((0, 2 * unit * count - rows),) + ((0, 0),) * (value.ndim - 1))
    half = unit * count
    keep = lax.dynamic_slice_in_dim(buf, core * half, half, 0)
    send = lax.dynamic_slice_in_dim(buf, (1 - core) * half, half, 0)
    part = keep + lax.ppermute(send, "pxc", swap)
    pieces = part.reshape((count, unit) + value.shape[1:]).astype(jnp.bfloat16)
    got = lax.all_to_all(pieces, "pxa", 0, 0).astype(jnp.float32)
    mine = jnp.sum(got, axis=0).astype(jnp.bfloat16)
    spread = jnp.broadcast_to(mine[None], pieces.shape)
    ours = lax.all_to_all(spread, "pxa", 0, 0).reshape((half,) + value.shape[1:])
    theirs = lax.ppermute(ours, "pxc", swap)
    low = jnp.where(core == 0, ours, theirs)
    high = jnp.where(core == 0, theirs, ours)
    return jnp.concatenate([low, high], axis=0)[:rows].astype(jnp.float32)


def bin_charges(charge, hit_bins, hit_ticks):
    tick_hot = (hit_ticks[..., None] == jnp.arange(SHIFTS, dtype=jnp.int32)).astype(jnp.float32)
    bin_hot = (hit_bins[..., None] == jnp.arange(BINS, dtype=jnp.int32)).astype(jnp.float32)
    weighted = charge[..., None] * tick_hot
    return jnp.einsum("xyks,xykb->xysb", weighted, bin_hot).astype(jnp.bfloat16)


def gather_offsets(source, rows, cols, count_x, count_y):
    pieces = []
    for row_off in range(-2, 3):
        for col_off in range(-2, 3):
            partial_value = source[
                2 - row_off : 2 - row_off + count_x, 2 - col_off : 2 - col_off + count_y
            ]
            row_same = rows[2 - row_off : 2 - row_off + count_x] == rows[2 : 2 + count_x]
            col_same = cols[2 - col_off : 2 - col_off + count_y] == cols[2 : 2 + count_y]
            allowed = row_same[:, None] & col_same[None, :]
            pieces.append(
                jnp.where(
                    allowed[:, :, None, None], partial_value, jnp.zeros((), partial_value.dtype)
                )
            )
    return jnp.stack(pieces, 0)


def shift_sum(partial_value, ticks):
    total = jnp.zeros(partial_value.shape[:2] + (ticks + SHIFTS,), jnp.float32)
    for offset in range(SHIFTS):
        total = total + jnp.pad(
            partial_value[:, :, offset, :], ((0, 0), (0, 0), (offset, SHIFTS - offset))
        )
    return total


def windows(resid, ticks):
    return jnp.stack([resid[:, :, offset : offset + ticks] for offset in range(SHIFTS)], axis=2)


def residual_of(prediction, measured, active):
    return (
        (prediction - measured.astype(jnp.float32)) * active.astype(jnp.float32)[..., None]
    ).astype(jnp.bfloat16)


def on_device(table, charge, hit_bins, hit_ticks, active, measured, row_module, col_module):
    tile_x, tile_y = (charge.shape[0], charge.shape[1])
    ticks = table.shape[2]
    parts_y = lax.axis_size("py")
    share = ticks // parts_y
    span = share + SHIFTS - 1
    weights = table.astype(jnp.bfloat16)
    row_start = px_index() * tile_x
    col_start = lax.axis_index("py") * tile_y

    deposits = jnp.stack(
        [charge, hit_bins.astype(jnp.float32), hit_ticks.astype(jnp.float32)], axis=-1
    )
    spread = jnp.broadcast_to(deposits[None], (parts_y,) + deposits.shape)
    band = jnp.transpose(lax.all_to_all(spread, "py", 0, 0), (1, 0, 2, 3, 4))
    band = band.reshape((tile_x, parts_y * tile_y) + deposits.shape[2:])
    above = passed_along(band[tile_x - 2 :], PX, 1)
    below = passed_along(band[:2], PX, -1)
    wide = jnp.concatenate([above, band, below], axis=0)
    binned = bin_charges(
        wide[..., 0], wide[..., 1].astype(jnp.int32), wide[..., 2].astype(jnp.int32)
    )
    source = jnp.pad(binned, ((0, 0), (2, 2), (0, 0), (0, 0)))
    width = source.shape[1] - 4
    rows_wide = lax.dynamic_slice_in_dim(
        jnp.pad(row_module, 2, constant_values=-1), row_start, tile_x + 4, 0
    )
    cols_all = jnp.pad(col_module, 2, constant_values=-1)

    own_source = lax.dynamic_slice_in_dim(source, col_start, tile_y + 4, 1)
    own_cols = lax.dynamic_slice_in_dim(cols_all, col_start, tile_y + 4, 0)
    stacked = gather_offsets(own_source, rows_wide, own_cols, tile_x, tile_y)
    partial_value = jnp.einsum(
        "oxysb,obt->xyst", stacked, weights, preferred_element_type=jnp.float32
    )
    prediction = shift_sum(partial_value, ticks)
    resid = residual_of(prediction, measured, active)

    sent = jnp.stack(
        [resid[:, :, k * share : k * share + span] for k in range(parts_y)], axis=0
    )
    got = lax.all_to_all(sent, "py", 0, 0)
    band_resid = jnp.transpose(got, (1, 0, 2, 3)).reshape(tile_x, width, span)

    stacked_band = gather_offsets(source, rows_wide, cols_all, tile_x, width)
    gradient = jnp.einsum(
        "oxysb,xysu->obu",
        stacked_band,
        windows(band_resid, share),
        preferred_element_type=jnp.float32,
    )
    flat = gradient.reshape(-1, share)
    summed = chip_sum(flat).reshape(gradient.shape)
    return (prediction.astype(jnp.bfloat16), summed / 16)


def solution(mesh):
    in_specs = (
        P(),
        P("px", "py", None),
        P("px", "py", None),
        P("px", "py", None),
        P("px", "py"),
        P("px", "py", None),
        P(),
        P(),
    )
    out_specs = (P("px", "py", None), P(None, None, "py"))
    rows_of = mesh.shape["px"]
    split = jax.sharding.Mesh(
        mesh.devices.reshape((rows_of // 2, 2) + mesh.devices.shape[1:]), ("pxa", "pxc", "py")
    )
    rename = lambda spec: P(*[PX if part == "px" else part for part in spec])
    return jax.shard_map(
        on_device,
        mesh=split,
        in_specs=tuple(rename(spec) for spec in in_specs),
        out_specs=tuple(rename(spec) for spec in out_specs),
        check_vma=False,
    )
```

```python
import jax
import jax.numpy as jnp
from jax import lax
from jax.sharding import PartitionSpec as P

BINS = 50
SHIFTS = 24
PX = ("pza", "pxh", "pxc")


def px_index():
    return lax.axis_index("pza") * 4 + lax.axis_index("pxh") * 2 + lax.axis_index("pxc")


def passed_along(block, axis, distance):
    devices = range(lax.axis_size("pza") * 4)
    route = [(i - distance, i) for i in devices if i - distance in devices]
    return lax.ppermute(block, axis, route)


def tree_sum(value, axis):
    count = lax.axis_size(axis)
    me = lax.axis_index(axis)
    steps = count.bit_length() - 1
    rows = value.shape[0]
    unit = -(-rows // count)
    buf = jnp.pad(value, ((0, unit * count - rows),) + ((0, 0),) * (value.ndim - 1))
    bits = []
    for k in range(steps):
        gap = 1 << k
        bit = (me >> k) & 1
        bits.append(bit)
        half = buf.shape[0] // 2
        keep = lax.dynamic_slice_in_dim(buf, bit * half, half, 0)
        send = lax.dynamic_slice_in_dim(buf, (1 - bit) * half, half, 0)
        got = lax.ppermute(send, axis, [(p, p ^ gap) for p in range(count)])
        buf = keep + got
    for k in reversed(range(steps)):
        gap = 1 << k
        got = lax.ppermute(buf, axis, [(p, p ^ gap) for p in range(count)])
        low = jnp.where(bits[k] == 0, buf, got)
        high = jnp.where(bits[k] == 0, got, buf)
        buf = jnp.concatenate([low, high], axis=0)
    return buf[:rows]


def exchange_sum(value, axis):
    count = lax.axis_size(axis)
    rows = value.shape[0]
    unit = -(-rows // count)
    buf = jnp.pad(value, ((0, unit * count - rows),) + ((0, 0),) * (value.ndim - 1))
    pieces = buf.reshape((count, unit) + value.shape[1:])
    mine = jnp.sum(lax.all_to_all(pieces, axis, 0, 0), axis=0)
    spread = jnp.broadcast_to(mine[None], pieces.shape)
    every = lax.all_to_all(spread, axis, 0, 0)
    return every.reshape(buf.shape)[:rows]


def chip_sum(value):
    swap = [(0, 1), (1, 0)]
    count = lax.axis_size("pza")
    rows = value.shape[0]
    unit = -(-rows // (4 * count))
    buf = jnp.pad(value, ((0, 4 * unit * count - rows),) + ((0, 0),) * (value.ndim - 1))
    sides = []
    for axis in ("pxc", "pxh"):
        side = lax.axis_index(axis)
        sides.append(side)
        half = buf.shape[0] // 2
        keep = lax.dynamic_slice_in_dim(buf, side * half, half, 0)
        send = lax.dynamic_slice_in_dim(buf, (1 - side) * half, half, 0)
        if axis != "pxc":
            send = send.astype(jnp.bfloat16)
        buf = keep + lax.ppermute(send, axis, swap).astype(jnp.float32)
    pieces = buf.reshape((count, unit) + value.shape[1:]).astype(jnp.bfloat16)
    got = lax.all_to_all(pieces, "pza", 0, 0).astype(jnp.float32)
    mine = jnp.sum(got, axis=0).astype(jnp.bfloat16)
    spread = jnp.broadcast_to(mine[None], pieces.shape)
    ours = lax.all_to_all(spread, "pza", 0, 0).reshape((count * unit,) + value.shape[1:])
    for axis, side in zip(("pxh", "pxc"), reversed(sides)):
        theirs = lax.ppermute(ours, axis, swap)
        low = jnp.where(side == 0, ours, theirs)
        high = jnp.where(side == 0, theirs, ours)
        ours = jnp.concatenate([low, high], axis=0)
    return ours[:rows].astype(jnp.float32)


def bin_charges(charge, hit_bins, hit_ticks):
    tick_hot = (hit_ticks[..., None] == jnp.arange(SHIFTS, dtype=jnp.int32)).astype(jnp.float32)
    bin_hot = (hit_bins[..., None] == jnp.arange(BINS, dtype=jnp.int32)).astype(jnp.float32)
    weighted = charge[..., None] * tick_hot
    return jnp.einsum("xyks,xykb->xysb", weighted, bin_hot).astype(jnp.bfloat16)


def gather_offsets(source, rows, cols, count_x, count_y):
    pieces = []
    for row_off in range(-2, 3):
        for col_off in range(-2, 3):
            partial_value = source[
                2 - row_off : 2 - row_off + count_x, 2 - col_off : 2 - col_off + count_y
            ]
            row_same = rows[2 - row_off : 2 - row_off + count_x] == rows[2 : 2 + count_x]
            col_same = cols[2 - col_off : 2 - col_off + count_y] == cols[2 : 2 + count_y]
            allowed = row_same[:, None] & col_same[None, :]
            pieces.append(
                jnp.where(
                    allowed[:, :, None, None], partial_value, jnp.zeros((), partial_value.dtype)
                )
            )
    return jnp.stack(pieces, 0)


def shift_sum(partial_value, ticks):
    total = jnp.zeros(partial_value.shape[:2] + (ticks + SHIFTS,), jnp.float32)
    for offset in range(SHIFTS):
        total = total + jnp.pad(
            partial_value[:, :, offset, :], ((0, 0), (0, 0), (offset, SHIFTS - offset))
        )
    return total


def windows(resid, ticks):
    return jnp.stack([resid[:, :, offset : offset + ticks] for offset in range(SHIFTS)], axis=2)


def residual_of(prediction, measured, active):
    return (
        (prediction - measured.astype(jnp.float32)) * active.astype(jnp.float32)[..., None]
    ).astype(jnp.bfloat16)


def on_device(table, charge, hit_bins, hit_ticks, active, measured, row_module, col_module):
    tile_x, tile_y = (charge.shape[0], charge.shape[1])
    ticks = table.shape[2]
    parts_y = lax.axis_size("py")
    share = ticks // parts_y
    span = share + SHIFTS - 1
    weights = table.astype(jnp.bfloat16)
    row_start = px_index() * tile_x
    col_start = lax.axis_index("py") * tile_y

    deposits = jnp.stack(
        [charge, hit_bins.astype(jnp.float32), hit_ticks.astype(jnp.float32)], axis=-1
    )
    spread = jnp.broadcast_to(deposits[None], (parts_y,) + deposits.shape)
    band = jnp.transpose(lax.all_to_all(spread, "py", 0, 0), (1, 0, 2, 3, 4))
    band = band.reshape((tile_x, parts_y * tile_y) + deposits.shape[2:])
    above = passed_along(band[tile_x - 2 :], PX, 1)
    below = passed_along(band[:2], PX, -1)
    wide = jnp.concatenate([above, band, below], axis=0)
    binned = bin_charges(
        wide[..., 0], wide[..., 1].astype(jnp.int32), wide[..., 2].astype(jnp.int32)
    )
    source = jnp.pad(binned, ((0, 0), (2, 2), (0, 0), (0, 0)))
    width = source.shape[1] - 4
    rows_wide = lax.dynamic_slice_in_dim(
        jnp.pad(row_module, 2, constant_values=-1), row_start, tile_x + 4, 0
    )
    cols_all = jnp.pad(col_module, 2, constant_values=-1)

    own_source = lax.dynamic_slice_in_dim(source, col_start, tile_y + 4, 1)
    own_cols = lax.dynamic_slice_in_dim(cols_all, col_start, tile_y + 4, 0)
    stacked = gather_offsets(own_source, rows_wide, own_cols, tile_x, tile_y)
    partial_value = jnp.einsum(
        "oxysb,obt->xyst", stacked, weights, preferred_element_type=jnp.float32
    )
    prediction = shift_sum(partial_value, ticks)
    resid = residual_of(prediction, measured, active)

    sent = jnp.stack(
        [resid[:, :, k * share : k * share + span] for k in range(parts_y)], axis=0
    )
    got = lax.all_to_all(sent, "py", 0, 0)
    band_resid = jnp.transpose(got, (1, 0, 2, 3)).reshape(tile_x, width, span)

    stacked_band = gather_offsets(source, rows_wide, cols_all, tile_x, width)
    gradient = jnp.einsum(
        "oxysb,xysu->obu",
        stacked_band,
        windows(band_resid, share),
        preferred_element_type=jnp.float32,
    )
    flat = gradient.reshape(-1, share)
    summed = chip_sum(flat).reshape(gradient.shape)
    return (prediction.astype(jnp.bfloat16), summed / 16)


def solution(mesh):
    in_specs = (
        P(),
        P("px", "py", None),
        P("px", "py", None),
        P("px", "py", None),
        P("px", "py"),
        P("px", "py", None),
        P(),
        P(),
    )
    out_specs = (P("px", "py", None), P(None, None, "py"))
    rows_of = mesh.shape["px"]
    split = jax.sharding.Mesh(
        mesh.devices.reshape((rows_of // 4, 2, 2) + mesh.devices.shape[1:]),
        ("pza", "pxh", "pxc", "py"),
    )
    rename = lambda spec: P(*[PX if part == "px" else part for part in spec])
    return jax.shard_map(
        on_device,
        mesh=split,
        in_specs=tuple(rename(spec) for spec in in_specs),
        out_specs=tuple(rename(spec) for spec in out_specs),
        check_vma=False,
    )
```

```python
import jax
import jax.numpy as jnp
from jax import lax
from jax.sharding import PartitionSpec as P

BINS = 50
SHIFTS = 24
PX = ("pxa", "pxc")


def px_index():
    return lax.axis_index("pxa") * 2 + lax.axis_index("pxc")


def passed_along(block, axis, distance):
    devices = range(lax.axis_size("pxa") * 2)
    route = [(i - distance, i) for i in devices if i - distance in devices]
    return lax.ppermute(block, axis, route)


def tree_sum(value, axis):
    count = lax.axis_size(axis)
    me = lax.axis_index(axis)
    steps = count.bit_length() - 1
    rows = value.shape[0]
    unit = -(-rows // count)
    buf = jnp.pad(value, ((0, unit * count - rows),) + ((0, 0),) * (value.ndim - 1))
    bits = []
    for k in range(steps):
        gap = 1 << k
        bit = (me >> k) & 1
        bits.append(bit)
        half = buf.shape[0] // 2
        keep = lax.dynamic_slice_in_dim(buf, bit * half, half, 0)
        send = lax.dynamic_slice_in_dim(buf, (1 - bit) * half, half, 0)
        got = lax.ppermute(send, axis, [(p, p ^ gap) for p in range(count)])
        buf = keep + got
    for k in reversed(range(steps)):
        gap = 1 << k
        got = lax.ppermute(buf, axis, [(p, p ^ gap) for p in range(count)])
        low = jnp.where(bits[k] == 0, buf, got)
        high = jnp.where(bits[k] == 0, got, buf)
        buf = jnp.concatenate([low, high], axis=0)
    return buf[:rows]


def exchange_sum(value, axis):
    count = lax.axis_size(axis)
    rows = value.shape[0]
    unit = -(-rows // count)
    buf = jnp.pad(value, ((0, unit * count - rows),) + ((0, 0),) * (value.ndim - 1))
    pieces = buf.reshape((count, unit) + value.shape[1:])
    mine = jnp.sum(lax.all_to_all(pieces, axis, 0, 0), axis=0)
    spread = jnp.broadcast_to(mine[None], pieces.shape)
    every = lax.all_to_all(spread, axis, 0, 0)
    return every.reshape(buf.shape)[:rows]


def chip_sum(value):
    count = lax.axis_size("pxa")
    core = lax.axis_index("pxc")
    swap = [(0, 1), (1, 0)]
    rows = value.shape[0]
    unit = -(-rows // (2 * count))
    buf = jnp.pad(value, ((0, 2 * unit * count - rows),) + ((0, 0),) * (value.ndim - 1))
    half = unit * count
    keep = lax.dynamic_slice_in_dim(buf, core * half, half, 0)
    send = lax.dynamic_slice_in_dim(buf, (1 - core) * half, half, 0)
    part = keep + lax.ppermute(send, "pxc", swap)
    pieces = part.reshape((count, unit) + value.shape[1:]).astype(jnp.bfloat16)
    got = lax.all_to_all(pieces, "pxa", 0, 0).astype(jnp.float32)
    mine = jnp.sum(got, axis=0).astype(jnp.bfloat16)
    spread = jnp.broadcast_to(mine[None], pieces.shape)
    ours = lax.all_to_all(spread, "pxa", 0, 0).reshape((half,) + value.shape[1:])
    theirs = lax.ppermute(ours, "pxc", swap)
    low = jnp.where(core == 0, ours, theirs)
    high = jnp.where(core == 0, theirs, ours)
    return jnp.concatenate([low, high], axis=0)[:rows].astype(jnp.float32)


def bin_charges(charge, hit_bins, hit_ticks):
    tick_hot = (hit_ticks[..., None] == jnp.arange(SHIFTS, dtype=jnp.int32)).astype(jnp.float32)
    bin_hot = (hit_bins[..., None] == jnp.arange(BINS, dtype=jnp.int32)).astype(jnp.float32)
    weighted = charge[..., None] * tick_hot
    return jnp.einsum("xyks,xykb->xysb", weighted, bin_hot).astype(jnp.bfloat16)


def bin_sum(charge, hit_bins, hit_ticks):
    total = jnp.zeros(charge.shape[:2] + (SHIFTS, BINS), jnp.float32)
    ticks = jnp.arange(SHIFTS, dtype=jnp.int32)[:, None]
    bins = jnp.arange(BINS, dtype=jnp.int32)[None, :]
    for k in range(charge.shape[2]):
        hit = (hit_ticks[:, :, k, None, None] == ticks) & (hit_bins[:, :, k, None, None] == bins)
        total = total + jnp.where(hit, charge[:, :, k, None, None], 0.0)
    return total.astype(jnp.bfloat16)


def gather_offsets(source, rows, cols, count_x, count_y):
    pieces = []
    for row_off in range(-2, 3):
        for col_off in range(-2, 3):
            partial_value = source[
                2 - row_off : 2 - row_off + count_x, 2 - col_off : 2 - col_off + count_y
            ]
            row_same = rows[2 - row_off : 2 - row_off + count_x] == rows[2 : 2 + count_x]
            col_same = cols[2 - col_off : 2 - col_off + count_y] == cols[2 : 2 + count_y]
            allowed = row_same[:, None] & col_same[None, :]
            pieces.append(
                jnp.where(
                    allowed[:, :, None, None], partial_value, jnp.zeros((), partial_value.dtype)
                )
            )
    return jnp.stack(pieces, 0)


def shift_sum(partial_value, ticks):
    total = jnp.zeros(partial_value.shape[:2] + (ticks + SHIFTS,), jnp.float32)
    for offset in range(SHIFTS):
        total = total + jnp.pad(
            partial_value[:, :, offset, :], ((0, 0), (0, 0), (offset, SHIFTS - offset))
        )
    return total


def windows(resid, ticks):
    return jnp.stack([resid[:, :, offset : offset + ticks] for offset in range(SHIFTS)], axis=2)


def residual_of(prediction, measured, active):
    return (
        (prediction - measured.astype(jnp.float32)) * active.astype(jnp.float32)[..., None]
    ).astype(jnp.bfloat16)


def on_device(table, charge, hit_bins, hit_ticks, active, measured, row_module, col_module):
    tile_x, tile_y = (charge.shape[0], charge.shape[1])
    ticks = table.shape[2]
    parts_y = lax.axis_size("py")
    share = ticks // parts_y
    span = share + SHIFTS - 1
    weights = table.astype(jnp.bfloat16)
    row_start = px_index() * tile_x
    col_start = lax.axis_index("py") * tile_y

    deposits = jnp.stack(
        [charge, hit_bins.astype(jnp.float32), hit_ticks.astype(jnp.float32)], axis=-1
    )
    spread = jnp.broadcast_to(deposits[None], (parts_y,) + deposits.shape)
    band = jnp.transpose(lax.all_to_all(spread, "py", 0, 0), (1, 0, 2, 3, 4))
    band = band.reshape((tile_x, parts_y * tile_y) + deposits.shape[2:])
    above = passed_along(band[tile_x - 2 :], PX, 1)
    below = passed_along(band[:2], PX, -1)
    wide = jnp.concatenate([above, band, below], axis=0)
    binned = bin_sum(
        wide[..., 0], wide[..., 1].astype(jnp.int32), wide[..., 2].astype(jnp.int32)
    )
    source = jnp.pad(binned, ((0, 0), (2, 2), (0, 0), (0, 0)))
    width = source.shape[1] - 4
    rows_wide = lax.dynamic_slice_in_dim(
        jnp.pad(row_module, 2, constant_values=-1), row_start, tile_x + 4, 0
    )
    cols_all = jnp.pad(col_module, 2, constant_values=-1)

    own_source = lax.dynamic_slice_in_dim(source, col_start, tile_y + 4, 1)
    own_cols = lax.dynamic_slice_in_dim(cols_all, col_start, tile_y + 4, 0)
    stacked = gather_offsets(own_source, rows_wide, own_cols, tile_x, tile_y)
    partial_value = jnp.einsum(
        "oxysb,obt->xyst", stacked, weights, preferred_element_type=jnp.float32
    )
    prediction = shift_sum(partial_value, ticks)
    resid = residual_of(prediction, measured, active)

    room = jnp.pad(resid, ((0, 0), (0, 0), (0, (parts_y + 1) * share - resid.shape[2])))
    lead = room[:, :, : parts_y * share].reshape(tile_x, tile_y, parts_y, share)
    rest = room[:, :, share : (parts_y + 1) * share].reshape(tile_x, tile_y, parts_y, share)
    sent = jnp.moveaxis(jnp.concatenate([lead, rest[..., : span - share]], axis=-1), 2, 0)
    got = lax.all_to_all(sent, "py", 0, 0)
    band_resid = jnp.transpose(got, (1, 0, 2, 3)).reshape(tile_x, width, span)

    stacked_band = gather_offsets(source, rows_wide, cols_all, tile_x, width)
    gradient = jnp.einsum(
        "oxysb,xysu->obu",
        stacked_band,
        windows(band_resid, share),
        preferred_element_type=jnp.float32,
    )
    flat = gradient.reshape(-1, share)
    summed = chip_sum(flat).reshape(gradient.shape)
    return (prediction.astype(jnp.bfloat16), summed / 16)


def solution(mesh):
    in_specs = (
        P(),
        P("px", "py", None),
        P("px", "py", None),
        P("px", "py", None),
        P("px", "py"),
        P("px", "py", None),
        P(),
        P(),
    )
    out_specs = (P("px", "py", None), P(None, None, "py"))
    rows_of = mesh.shape["px"]
    split = jax.sharding.Mesh(
        mesh.devices.reshape((rows_of // 2, 2) + mesh.devices.shape[1:]), ("pxa", "pxc", "py")
    )
    rename = lambda spec: P(*[PX if part == "px" else part for part in spec])
    return jax.shard_map(
        on_device,
        mesh=split,
        in_specs=tuple(rename(spec) for spec in in_specs),
        out_specs=tuple(rename(spec) for spec in out_specs),
        check_vma=False,
    )
```

```python
import jax
import jax.numpy as jnp
from jax import lax
from jax.sharding import PartitionSpec as P

BINS = 50
SHIFTS = 24
PX = ("pxa", "pxc")


def px_index():
    return lax.axis_index("pxa") * 2 + lax.axis_index("pxc")


def passed_along(block, axis, distance):
    devices = range(lax.axis_size("pxa") * 2)
    route = [(i - distance, i) for i in devices if i - distance in devices]
    return lax.ppermute(block, axis, route)


def tree_sum(value, axis):
    count = lax.axis_size(axis)
    me = lax.axis_index(axis)
    steps = count.bit_length() - 1
    rows = value.shape[0]
    unit = -(-rows // count)
    buf = jnp.pad(value, ((0, unit * count - rows),) + ((0, 0),) * (value.ndim - 1))
    bits = []
    for k in range(steps):
        gap = 1 << k
        bit = (me >> k) & 1
        bits.append(bit)
        half = buf.shape[0] // 2
        keep = lax.dynamic_slice_in_dim(buf, bit * half, half, 0)
        send = lax.dynamic_slice_in_dim(buf, (1 - bit) * half, half, 0)
        got = lax.ppermute(send, axis, [(p, p ^ gap) for p in range(count)])
        buf = keep + got
    for k in reversed(range(steps)):
        gap = 1 << k
        got = lax.ppermute(buf, axis, [(p, p ^ gap) for p in range(count)])
        low = jnp.where(bits[k] == 0, buf, got)
        high = jnp.where(bits[k] == 0, got, buf)
        buf = jnp.concatenate([low, high], axis=0)
    return buf[:rows]


def exchange_sum(value, axis):
    count = lax.axis_size(axis)
    rows = value.shape[0]
    unit = -(-rows // count)
    buf = jnp.pad(value, ((0, unit * count - rows),) + ((0, 0),) * (value.ndim - 1))
    pieces = buf.reshape((count, unit) + value.shape[1:])
    mine = jnp.sum(lax.all_to_all(pieces, axis, 0, 0), axis=0)
    spread = jnp.broadcast_to(mine[None], pieces.shape)
    every = lax.all_to_all(spread, axis, 0, 0)
    return every.reshape(buf.shape)[:rows]


def chip_sum(value):
    count = lax.axis_size("pxa")
    core = lax.axis_index("pxc")
    swap = [(0, 1), (1, 0)]
    rows = value.shape[0]
    unit = -(-rows // (2 * count))
    buf = jnp.pad(value, ((0, 2 * unit * count - rows),) + ((0, 0),) * (value.ndim - 1))
    half = unit * count
    keep = lax.dynamic_slice_in_dim(buf, core * half, half, 0)
    send = lax.dynamic_slice_in_dim(buf, (1 - core) * half, half, 0)
    part = keep + lax.ppermute(send, "pxc", swap)
    pieces = part.reshape((count, unit) + value.shape[1:]).astype(jnp.bfloat16)
    got = lax.all_to_all(pieces, "pxa", 0, 0).astype(jnp.float32)
    mine = jnp.sum(got, axis=0).astype(jnp.bfloat16)
    spread = jnp.broadcast_to(mine[None], pieces.shape)
    ours = lax.all_to_all(spread, "pxa", 0, 0).reshape((half,) + value.shape[1:])
    theirs = lax.ppermute(ours, "pxc", swap)
    low = jnp.where(core == 0, ours, theirs)
    high = jnp.where(core == 0, theirs, ours)
    return jnp.concatenate([low, high], axis=0)[:rows].astype(jnp.float32)


def bin_charges(charge, hit_bins, hit_ticks):
    tick_hot = (hit_ticks[..., None] == jnp.arange(SHIFTS, dtype=jnp.int32)).astype(jnp.float32)
    bin_hot = (hit_bins[..., None] == jnp.arange(BINS, dtype=jnp.int32)).astype(jnp.float32)
    weighted = charge[..., None] * tick_hot
    return jnp.einsum("xyks,xykb->xysb", weighted, bin_hot).astype(jnp.bfloat16)


def gather_offsets(source, rows, cols, count_x, count_y):
    pieces = []
    for row_off in range(-2, 3):
        for col_off in range(-2, 3):
            partial_value = source[
                2 - row_off : 2 - row_off + count_x, 2 - col_off : 2 - col_off + count_y
            ]
            row_same = rows[2 - row_off : 2 - row_off + count_x] == rows[2 : 2 + count_x]
            col_same = cols[2 - col_off : 2 - col_off + count_y] == cols[2 : 2 + count_y]
            allowed = row_same[:, None] & col_same[None, :]
            pieces.append(
                jnp.where(
                    allowed[:, :, None, None], partial_value, jnp.zeros((), partial_value.dtype)
                )
            )
    return jnp.stack(pieces, 0)


def shift_sum(partial_value, ticks):
    total = jnp.zeros(partial_value.shape[:2] + (ticks + SHIFTS,), jnp.float32)
    for offset in range(SHIFTS):
        total = total + jnp.pad(
            partial_value[:, :, offset, :], ((0, 0), (0, 0), (offset, SHIFTS - offset))
        )
    return total


def windows(resid, ticks):
    return jnp.stack([resid[:, :, offset : offset + ticks] for offset in range(SHIFTS)], axis=2)


def residual_of(prediction, measured, active):
    return (
        (prediction - measured.astype(jnp.float32)) * active.astype(jnp.float32)[..., None]
    ).astype(jnp.bfloat16)


def on_device(table, charge, hit_bins, hit_ticks, active, measured, row_module, col_module):
    tile_x, tile_y = (charge.shape[0], charge.shape[1])
    ticks = table.shape[2]
    parts_y = lax.axis_size("py")
    share = ticks // parts_y
    span = share + SHIFTS - 1
    weights = table.astype(jnp.bfloat16)
    row_start = px_index() * tile_x
    col_start = lax.axis_index("py") * tile_y

    deposits = jnp.stack(
        [charge, hit_bins.astype(jnp.float32), hit_ticks.astype(jnp.float32)], axis=-1
    )
    spread = jnp.broadcast_to(deposits[None], (parts_y,) + deposits.shape)
    band = jnp.transpose(lax.all_to_all(spread, "py", 0, 0), (1, 0, 2, 3, 4))
    band = band.reshape((tile_x, parts_y * tile_y) + deposits.shape[2:])
    above = passed_along(band[tile_x - 2 :], PX, 1)
    below = passed_along(band[:2], PX, -1)
    wide = jnp.concatenate([above, band, below], axis=0)
    binned = bin_charges(
        wide[..., 0], wide[..., 1].astype(jnp.int32), wide[..., 2].astype(jnp.int32)
    )
    source = jnp.pad(binned, ((0, 0), (2, 2), (0, 0), (0, 0)))
    width = source.shape[1] - 4
    rows_wide = lax.dynamic_slice_in_dim(
        jnp.pad(row_module, 2, constant_values=-1), row_start, tile_x + 4, 0
    )
    cols_all = jnp.pad(col_module, 2, constant_values=-1)

    own_source = lax.dynamic_slice_in_dim(source, col_start, tile_y + 4, 1)
    own_cols = lax.dynamic_slice_in_dim(cols_all, col_start, tile_y + 4, 0)
    stacked = gather_offsets(own_source, rows_wide, own_cols, tile_x, tile_y)
    partial_value = jnp.einsum(
        "oxysb,obt->xyst", stacked, weights, preferred_element_type=jnp.float32
    )
    prediction = shift_sum(partial_value, ticks)
    resid = residual_of(prediction, measured, active)

    room = jnp.pad(resid, ((0, 0), (0, 0), (0, (parts_y + 1) * share - resid.shape[2])))
    lead = room[:, :, : parts_y * share].reshape(tile_x, tile_y, parts_y, share)
    rest = room[:, :, share : (parts_y + 1) * share].reshape(tile_x, tile_y, parts_y, share)
    sent = jnp.moveaxis(jnp.concatenate([lead, rest[..., : span - share]], axis=-1), 2, 0)
    got = lax.all_to_all(sent, "py", 0, 0)
    band_resid = jnp.transpose(got, (1, 0, 2, 3)).reshape(tile_x, width, span)

    stacked_band = gather_offsets(source, rows_wide, cols_all, tile_x, width)
    gradient = jnp.einsum(
        "oxysb,xysu->obu",
        stacked_band,
        windows(band_resid, share),
        preferred_element_type=jnp.float32,
    )
    flat = gradient.reshape(-1, share)
    summed = chip_sum(flat).reshape(gradient.shape)
    return (prediction.astype(jnp.bfloat16), summed / 16)


def solution(mesh):
    in_specs = (
        P(),
        P("px", "py", None),
        P("px", "py", None),
        P("px", "py", None),
        P("px", "py"),
        P("px", "py", None),
        P(),
        P(),
    )
    out_specs = (P("px", "py", None), P(None, None, "py"))
    rows_of = mesh.shape["px"]
    split = jax.sharding.Mesh(
        mesh.devices.reshape((rows_of // 2, 2) + mesh.devices.shape[1:]), ("pxa", "pxc", "py")
    )
    rename = lambda spec: P(*[PX if part == "px" else part for part in spec])
    return jax.shard_map(
        on_device,
        mesh=split,
        in_specs=tuple(rename(spec) for spec in in_specs),
        out_specs=tuple(rename(spec) for spec in out_specs),
        check_vma=False,
    )
```

```python
import jax
import jax.numpy as jnp
from jax import lax
from jax.sharding import PartitionSpec as P

BINS = 50
SHIFTS = 24
PX = ("pxa", "pxc")


def px_index():
    return lax.axis_index("pxa") * 2 + lax.axis_index("pxc")


def passed_along(block, axis, distance):
    devices = range(lax.axis_size("pxa") * 2)
    route = [(i - distance, i) for i in devices if i - distance in devices]
    return lax.ppermute(block, axis, route)


def tree_sum(value, axis):
    count = lax.axis_size(axis)
    me = lax.axis_index(axis)
    steps = count.bit_length() - 1
    rows = value.shape[0]
    unit = -(-rows // count)
    buf = jnp.pad(value, ((0, unit * count - rows),) + ((0, 0),) * (value.ndim - 1))
    bits = []
    for k in range(steps):
        gap = 1 << k
        bit = (me >> k) & 1
        bits.append(bit)
        half = buf.shape[0] // 2
        keep = lax.dynamic_slice_in_dim(buf, bit * half, half, 0)
        send = lax.dynamic_slice_in_dim(buf, (1 - bit) * half, half, 0)
        got = lax.ppermute(send, axis, [(p, p ^ gap) for p in range(count)])
        buf = keep + got
    for k in reversed(range(steps)):
        gap = 1 << k
        got = lax.ppermute(buf, axis, [(p, p ^ gap) for p in range(count)])
        low = jnp.where(bits[k] == 0, buf, got)
        high = jnp.where(bits[k] == 0, got, buf)
        buf = jnp.concatenate([low, high], axis=0)
    return buf[:rows]


def exchange_sum(value, axis):
    count = lax.axis_size(axis)
    rows = value.shape[0]
    unit = -(-rows // count)
    buf = jnp.pad(value, ((0, unit * count - rows),) + ((0, 0),) * (value.ndim - 1))
    pieces = buf.reshape((count, unit) + value.shape[1:])
    mine = jnp.sum(lax.all_to_all(pieces, axis, 0, 0), axis=0)
    spread = jnp.broadcast_to(mine[None], pieces.shape)
    every = lax.all_to_all(spread, axis, 0, 0)
    return every.reshape(buf.shape)[:rows]


def chip_sum(value):
    count = lax.axis_size("pxa")
    core = lax.axis_index("pxc")
    swap = [(0, 1), (1, 0)]
    rows = value.shape[0]
    unit = -(-rows // (2 * count))
    buf = jnp.pad(value, ((0, 2 * unit * count - rows),) + ((0, 0),) * (value.ndim - 1))
    half = unit * count
    keep = lax.dynamic_slice_in_dim(buf, core * half, half, 0)
    send = lax.dynamic_slice_in_dim(buf, (1 - core) * half, half, 0)
    part = keep + lax.ppermute(send, "pxc", swap)
    pieces = part.reshape((count, unit) + value.shape[1:]).astype(jnp.bfloat16)
    got = lax.all_to_all(pieces, "pxa", 0, 0).astype(jnp.float32)
    mine = jnp.sum(got, axis=0).astype(jnp.bfloat16)
    spread = jnp.broadcast_to(mine[None], pieces.shape)
    ours = lax.all_to_all(spread, "pxa", 0, 0).reshape((half,) + value.shape[1:])
    theirs = lax.ppermute(ours, "pxc", swap)
    low = jnp.where(core == 0, ours, theirs)
    high = jnp.where(core == 0, theirs, ours)
    return jnp.concatenate([low, high], axis=0)[:rows].astype(jnp.float32)


def bin_charges(charge, hit_bins, hit_ticks):
    tick_hot = (hit_ticks[..., None] == jnp.arange(SHIFTS, dtype=jnp.int32)).astype(jnp.float32)
    bin_hot = (hit_bins[..., None] == jnp.arange(BINS, dtype=jnp.int32)).astype(jnp.float32)
    weighted = charge[..., None] * tick_hot
    return jnp.einsum("xyks,xykb->xysb", weighted, bin_hot).astype(jnp.bfloat16)


def gather_offsets(source, rows, cols, count_x, count_y):
    pieces = []
    for row_off in range(-2, 3):
        for col_off in range(-2, 3):
            partial_value = source[
                2 - row_off : 2 - row_off + count_x, 2 - col_off : 2 - col_off + count_y
            ]
            row_same = rows[2 - row_off : 2 - row_off + count_x] == rows[2 : 2 + count_x]
            col_same = cols[2 - col_off : 2 - col_off + count_y] == cols[2 : 2 + count_y]
            allowed = row_same[:, None] & col_same[None, :]
            pieces.append(
                jnp.where(
                    allowed[:, :, None, None], partial_value, jnp.zeros((), partial_value.dtype)
                )
            )
    return jnp.stack(pieces, 0)


def shift_sum(partial_value, ticks):
    total = jnp.zeros(partial_value.shape[:2] + (ticks + SHIFTS,), jnp.float32)
    for offset in range(SHIFTS):
        total = total + jnp.pad(
            partial_value[:, :, offset, :], ((0, 0), (0, 0), (offset, SHIFTS - offset))
        )
    return total


def windows(resid, ticks):
    return jnp.stack([resid[:, :, offset : offset + ticks] for offset in range(SHIFTS)], axis=2)


def residual_of(prediction, measured, active):
    return (
        (prediction - measured.astype(jnp.float32)) * active.astype(jnp.float32)[..., None]
    ).astype(jnp.bfloat16)


def on_device(table, charge, hit_bins, hit_ticks, active, measured, row_module, col_module):
    tile_x, tile_y = (charge.shape[0], charge.shape[1])
    ticks = table.shape[2]
    parts_y = lax.axis_size("py")
    share = ticks // parts_y
    span = share + SHIFTS - 1
    weights = table.astype(jnp.bfloat16)
    row_start = px_index() * tile_x
    col_start = lax.axis_index("py") * tile_y

    deposits = jnp.stack(
        [charge, hit_bins.astype(jnp.float32), hit_ticks.astype(jnp.float32)], axis=-1
    )
    spread = jnp.broadcast_to(deposits[None], (parts_y,) + deposits.shape)
    band = jnp.transpose(lax.all_to_all(spread, "py", 0, 0), (1, 0, 2, 3, 4))
    band = band.reshape((tile_x, parts_y * tile_y) + deposits.shape[2:])
    above = passed_along(band[tile_x - 2 :], PX, 1)
    below = passed_along(band[:2], PX, -1)
    wide = jnp.concatenate([above, band, below], axis=0)
    binned = bin_charges(
        wide[..., 0], wide[..., 1].astype(jnp.int32), wide[..., 2].astype(jnp.int32)
    )
    source = jnp.pad(binned, ((0, 0), (2, 2), (0, 0), (0, 0)))
    width = source.shape[1] - 4
    rows_wide = lax.dynamic_slice_in_dim(
        jnp.pad(row_module, 2, constant_values=-1), row_start, tile_x + 4, 0
    )
    cols_all = jnp.pad(col_module, 2, constant_values=-1)

    own_source = lax.dynamic_slice_in_dim(source, col_start, tile_y + 4, 1)
    own_cols = lax.dynamic_slice_in_dim(cols_all, col_start, tile_y + 4, 0)
    stacked = gather_offsets(own_source, rows_wide, own_cols, tile_x, tile_y)
    partial_value = jnp.einsum(
        "oxysb,obt->xyst", stacked, weights, preferred_element_type=jnp.float32
    )
    prediction = shift_sum(partial_value, ticks)
    resid = residual_of(prediction, measured, active)

    room = jnp.pad(resid, ((0, 0), (0, 0), (0, (parts_y + 1) * share - resid.shape[2])))
    lead = room[:, :, : parts_y * share].reshape(tile_x, tile_y, parts_y, share)
    rest = room[:, :, share : (parts_y + 1) * share].reshape(tile_x, tile_y, parts_y, share)
    sent = jnp.moveaxis(jnp.concatenate([lead, rest[..., : span - share]], axis=-1), 2, 0)
    got = lax.all_to_all(sent, "py", 0, 0)
    band_resid = jnp.transpose(got, (1, 0, 2, 3)).reshape(tile_x, width, span)

    stacked_band = gather_offsets(source, rows_wide, cols_all, tile_x, width)
    shifted = windows(band_resid, share)
    group = (stacked_band.shape[0] + 1) // 2
    sums = []
    for part in (stacked_band[:group], stacked_band[group:]):
        gradient = jnp.einsum(
            "oxysb,xysu->obu", part, shifted, preferred_element_type=jnp.float32
        )
        sums.append(chip_sum(gradient.reshape(-1, share)).reshape(gradient.shape))
    summed = jnp.concatenate(sums, axis=0)
    return (prediction.astype(jnp.bfloat16), summed / 16)


def solution(mesh):
    in_specs = (
        P(),
        P("px", "py", None),
        P("px", "py", None),
        P("px", "py", None),
        P("px", "py"),
        P("px", "py", None),
        P(),
        P(),
    )
    out_specs = (P("px", "py", None), P(None, None, "py"))
    rows_of = mesh.shape["px"]
    split = jax.sharding.Mesh(
        mesh.devices.reshape((rows_of // 2, 2) + mesh.devices.shape[1:]), ("pxa", "pxc", "py")
    )
    rename = lambda spec: P(*[PX if part == "px" else part for part in spec])
    return jax.shard_map(
        on_device,
        mesh=split,
        in_specs=tuple(rename(spec) for spec in in_specs),
        out_specs=tuple(rename(spec) for spec in out_specs),
        check_vma=False,
    )
```

```python
import jax
import jax.numpy as jnp
from jax import lax
from jax.sharding import PartitionSpec as P

BINS = 50
SHIFTS = 24
PX = ("pxa", "pxc")


def px_index():
    return lax.axis_index("pxa") * 2 + lax.axis_index("pxc")


def passed_along(block, axis, distance):
    devices = range(lax.axis_size("pxa") * 2)
    route = [(i - distance, i) for i in devices if i - distance in devices]
    return lax.ppermute(block, axis, route)


def tree_sum(value, axis):
    count = lax.axis_size(axis)
    me = lax.axis_index(axis)
    steps = count.bit_length() - 1
    rows = value.shape[0]
    unit = -(-rows // count)
    buf = jnp.pad(value, ((0, unit * count - rows),) + ((0, 0),) * (value.ndim - 1))
    bits = []
    for k in range(steps):
        gap = 1 << k
        bit = (me >> k) & 1
        bits.append(bit)
        half = buf.shape[0] // 2
        keep = lax.dynamic_slice_in_dim(buf, bit * half, half, 0)
        send = lax.dynamic_slice_in_dim(buf, (1 - bit) * half, half, 0)
        got = lax.ppermute(send, axis, [(p, p ^ gap) for p in range(count)])
        buf = keep + got
    for k in reversed(range(steps)):
        gap = 1 << k
        got = lax.ppermute(buf, axis, [(p, p ^ gap) for p in range(count)])
        low = jnp.where(bits[k] == 0, buf, got)
        high = jnp.where(bits[k] == 0, got, buf)
        buf = jnp.concatenate([low, high], axis=0)
    return buf[:rows]


def exchange_sum(value, axis):
    count = lax.axis_size(axis)
    rows = value.shape[0]
    unit = -(-rows // count)
    buf = jnp.pad(value, ((0, unit * count - rows),) + ((0, 0),) * (value.ndim - 1))
    pieces = buf.reshape((count, unit) + value.shape[1:])
    mine = jnp.sum(lax.all_to_all(pieces, axis, 0, 0), axis=0)
    spread = jnp.broadcast_to(mine[None], pieces.shape)
    every = lax.all_to_all(spread, axis, 0, 0)
    return every.reshape(buf.shape)[:rows]


def chip_sum(value):
    count = lax.axis_size("pxa")
    core = lax.axis_index("pxc")
    swap = [(0, 1), (1, 0)]
    rows = value.shape[0]
    unit = -(-rows // (2 * count))
    buf = jnp.pad(value, ((0, 2 * unit * count - rows),) + ((0, 0),) * (value.ndim - 1))
    half = unit * count
    keep = lax.dynamic_slice_in_dim(buf, core * half, half, 0)
    send = lax.dynamic_slice_in_dim(buf, (1 - core) * half, half, 0)
    part = keep + lax.ppermute(send, "pxc", swap)
    pieces = part.reshape((count, unit) + value.shape[1:]).astype(jnp.bfloat16)
    got = lax.all_to_all(pieces, "pxa", 0, 0).astype(jnp.float32)
    mine = jnp.sum(got, axis=0).astype(jnp.bfloat16)
    spread = jnp.broadcast_to(mine[None], pieces.shape)
    ours = lax.all_to_all(spread, "pxa", 0, 0).reshape((half,) + value.shape[1:])
    theirs = lax.ppermute(ours, "pxc", swap)
    low = jnp.where(core == 0, ours, theirs)
    high = jnp.where(core == 0, theirs, ours)
    return jnp.concatenate([low, high], axis=0)[:rows].astype(jnp.float32)


def bin_charges(charge, hit_bins, hit_ticks):
    tick_hot = (hit_ticks[..., None] == jnp.arange(SHIFTS, dtype=jnp.int32)).astype(jnp.float32)
    bin_hot = (hit_bins[..., None] == jnp.arange(BINS, dtype=jnp.int32)).astype(jnp.float32)
    weighted = charge[..., None] * tick_hot
    return jnp.einsum("xyks,xykb->xysb", weighted, bin_hot).astype(jnp.bfloat16)


def gather_offsets(source, rows, cols, count_x, count_y):
    pieces = []
    for row_off in range(-2, 3):
        for col_off in range(-2, 3):
            partial_value = source[
                2 - row_off : 2 - row_off + count_x, 2 - col_off : 2 - col_off + count_y
            ]
            row_same = rows[2 - row_off : 2 - row_off + count_x] == rows[2 : 2 + count_x]
            col_same = cols[2 - col_off : 2 - col_off + count_y] == cols[2 : 2 + count_y]
            allowed = row_same[:, None] & col_same[None, :]
            pieces.append(
                jnp.where(
                    allowed[:, :, None, None], partial_value, jnp.zeros((), partial_value.dtype)
                )
            )
    return jnp.stack(pieces, 0)


def shift_sum(partial_value, ticks):
    total = jnp.zeros(partial_value.shape[:2] + (ticks + SHIFTS,), jnp.float32)
    for offset in range(SHIFTS):
        total = total + jnp.pad(
            partial_value[:, :, offset, :], ((0, 0), (0, 0), (offset, SHIFTS - offset))
        )
    return total


def windows(resid, ticks):
    return jnp.stack([resid[:, :, offset : offset + ticks] for offset in range(SHIFTS)], axis=2)


def residual_of(prediction, measured, active):
    return (
        (prediction - measured.astype(jnp.float32)) * active.astype(jnp.float32)[..., None]
    ).astype(jnp.bfloat16)


def on_device(table, charge, hit_bins, hit_ticks, active, measured, row_module, col_module):
    tile_x, tile_y = (charge.shape[0], charge.shape[1])
    ticks = table.shape[2]
    parts_y = lax.axis_size("py")
    share = ticks // parts_y
    span = share + SHIFTS - 1
    weights = table.astype(jnp.bfloat16)
    row_start = px_index() * tile_x
    col_start = lax.axis_index("py") * tile_y

    deposits = jnp.stack(
        [charge, hit_bins.astype(jnp.float32), hit_ticks.astype(jnp.float32)], axis=-1
    )
    spread = jnp.broadcast_to(deposits[None], (parts_y,) + deposits.shape)
    band = jnp.transpose(lax.all_to_all(spread, "py", 0, 0), (1, 0, 2, 3, 4))
    band = band.reshape((tile_x, parts_y * tile_y) + deposits.shape[2:])
    above = passed_along(band[tile_x - 2 :], PX, 1)
    below = passed_along(band[:2], PX, -1)
    wide = jnp.concatenate([above, band, below], axis=0)
    binned = bin_charges(
        wide[..., 0], wide[..., 1].astype(jnp.int32), wide[..., 2].astype(jnp.int32)
    )
    source = jnp.pad(binned, ((0, 0), (2, 2), (0, 0), (0, 0)))
    width = source.shape[1] - 4
    rows_wide = lax.dynamic_slice_in_dim(
        jnp.pad(row_module, 2, constant_values=-1), row_start, tile_x + 4, 0
    )
    cols_all = jnp.pad(col_module, 2, constant_values=-1)

    stacked_band = gather_offsets(source, rows_wide, cols_all, tile_x, width)
    stacked = lax.dynamic_slice_in_dim(stacked_band, col_start, tile_y, 2)
    partial_value = jnp.einsum(
        "oxysb,obt->xyst", stacked, weights, preferred_element_type=jnp.float32
    )
    prediction = shift_sum(partial_value, ticks)
    resid = residual_of(prediction, measured, active)

    room = jnp.pad(resid, ((0, 0), (0, 0), (0, (parts_y + 1) * share - resid.shape[2])))
    lead = room[:, :, : parts_y * share].reshape(tile_x, tile_y, parts_y, share)
    rest = room[:, :, share : (parts_y + 1) * share].reshape(tile_x, tile_y, parts_y, share)
    sent = jnp.moveaxis(jnp.concatenate([lead, rest[..., : span - share]], axis=-1), 2, 0)
    got = lax.all_to_all(sent, "py", 0, 0)
    band_resid = jnp.transpose(got, (1, 0, 2, 3)).reshape(tile_x, width, span)

    gradient = jnp.einsum(
        "oxysb,xysu->obu",
        stacked_band,
        windows(band_resid, share),
        preferred_element_type=jnp.float32,
    )
    flat = gradient.reshape(-1, share)
    summed = chip_sum(flat).reshape(gradient.shape)
    return (prediction.astype(jnp.bfloat16), summed / 16)


def solution(mesh):
    in_specs = (
        P(),
        P("px", "py", None),
        P("px", "py", None),
        P("px", "py", None),
        P("px", "py"),
        P("px", "py", None),
        P(),
        P(),
    )
    out_specs = (P("px", "py", None), P(None, None, "py"))
    rows_of = mesh.shape["px"]
    split = jax.sharding.Mesh(
        mesh.devices.reshape((rows_of // 2, 2) + mesh.devices.shape[1:]), ("pxa", "pxc", "py")
    )
    rename = lambda spec: P(*[PX if part == "px" else part for part in spec])
    return jax.shard_map(
        on_device,
        mesh=split,
        in_specs=tuple(rename(spec) for spec in in_specs),
        out_specs=tuple(rename(spec) for spec in out_specs),
        check_vma=False,
    )
```

```python
import jax
import jax.numpy as jnp
from jax import lax
from jax.sharding import PartitionSpec as P

BINS = 50
SHIFTS = 24
PX = ("pxa", "pxc")


def px_index():
    return lax.axis_index("pxa") * 2 + lax.axis_index("pxc")


def passed_along(block, axis, distance):
    devices = range(lax.axis_size("pxa") * 2)
    route = [(i - distance, i) for i in devices if i - distance in devices]
    return lax.ppermute(block, axis, route)


def tree_sum(value, axis):
    count = lax.axis_size(axis)
    me = lax.axis_index(axis)
    steps = count.bit_length() - 1
    rows = value.shape[0]
    unit = -(-rows // count)
    buf = jnp.pad(value, ((0, unit * count - rows),) + ((0, 0),) * (value.ndim - 1))
    bits = []
    for k in range(steps):
        gap = 1 << k
        bit = (me >> k) & 1
        bits.append(bit)
        half = buf.shape[0] // 2
        keep = lax.dynamic_slice_in_dim(buf, bit * half, half, 0)
        send = lax.dynamic_slice_in_dim(buf, (1 - bit) * half, half, 0)
        got = lax.ppermute(send, axis, [(p, p ^ gap) for p in range(count)])
        buf = keep + got
    for k in reversed(range(steps)):
        gap = 1 << k
        got = lax.ppermute(buf, axis, [(p, p ^ gap) for p in range(count)])
        low = jnp.where(bits[k] == 0, buf, got)
        high = jnp.where(bits[k] == 0, got, buf)
        buf = jnp.concatenate([low, high], axis=0)
    return buf[:rows]


def exchange_sum(value, axis):
    count = lax.axis_size(axis)
    rows = value.shape[0]
    unit = -(-rows // count)
    buf = jnp.pad(value, ((0, unit * count - rows),) + ((0, 0),) * (value.ndim - 1))
    pieces = buf.reshape((count, unit) + value.shape[1:])
    mine = jnp.sum(lax.all_to_all(pieces, axis, 0, 0), axis=0)
    spread = jnp.broadcast_to(mine[None], pieces.shape)
    every = lax.all_to_all(spread, axis, 0, 0)
    return every.reshape(buf.shape)[:rows]


def chip_sum(value):
    count = lax.axis_size("pxa")
    core = lax.axis_index("pxc")
    swap = [(0, 1), (1, 0)]
    rows = value.shape[0]
    unit = -(-rows // (2 * count))
    buf = jnp.pad(value, ((0, 2 * unit * count - rows),) + ((0, 0),) * (value.ndim - 1))
    half = unit * count
    keep = lax.dynamic_slice_in_dim(buf, core * half, half, 0)
    send = lax.dynamic_slice_in_dim(buf, (1 - core) * half, half, 0)
    part = keep + lax.ppermute(send, "pxc", swap)
    pieces = part.reshape((count, unit) + value.shape[1:]).astype(jnp.bfloat16)
    got = lax.all_to_all(pieces, "pxa", 0, 0).astype(jnp.float32)
    mine = jnp.sum(got, axis=0).astype(jnp.bfloat16)
    spread = jnp.broadcast_to(mine[None], pieces.shape)
    ours = lax.all_to_all(spread, "pxa", 0, 0).reshape((half,) + value.shape[1:])
    theirs = lax.ppermute(ours, "pxc", swap)
    low = jnp.where(core == 0, ours, theirs)
    high = jnp.where(core == 0, theirs, ours)
    return jnp.concatenate([low, high], axis=0)[:rows].astype(jnp.float32)


def bin_charges(charge, hit_bins, hit_ticks):
    tick_hot = (hit_ticks[..., None] == jnp.arange(SHIFTS, dtype=jnp.int32)).astype(jnp.float32)
    bin_hot = (hit_bins[..., None] == jnp.arange(BINS, dtype=jnp.int32)).astype(jnp.float32)
    weighted = charge[..., None] * tick_hot
    return jnp.einsum("xyks,xykb->xysb", weighted, bin_hot).astype(jnp.bfloat16)


def gather_offsets(source, rows, cols, count_x, count_y):
    pieces = []
    for row_off in range(-2, 3):
        for col_off in range(-2, 3):
            partial_value = source[
                2 - row_off : 2 - row_off + count_x, 2 - col_off : 2 - col_off + count_y
            ]
            row_same = rows[2 - row_off : 2 - row_off + count_x] == rows[2 : 2 + count_x]
            col_same = cols[2 - col_off : 2 - col_off + count_y] == cols[2 : 2 + count_y]
            allowed = row_same[:, None] & col_same[None, :]
            pieces.append(
                jnp.where(
                    allowed[:, :, None, None], partial_value, jnp.zeros((), partial_value.dtype)
                )
            )
    return jnp.stack(pieces, 0)


def shift_sum(partial_value, ticks):
    total = jnp.zeros(partial_value.shape[:2] + (ticks + SHIFTS,), jnp.float32)
    for offset in range(SHIFTS):
        total = total + jnp.pad(
            partial_value[:, :, offset, :], ((0, 0), (0, 0), (offset, SHIFTS - offset))
        )
    return total


def windows(resid, ticks):
    return jnp.stack([resid[:, :, offset : offset + ticks] for offset in range(SHIFTS)], axis=2)


def toeplitz(resid, ticks):
    length = resid.shape[2]
    tiled = jnp.tile(resid, (1, 1, SHIFTS + 1))[:, :, : SHIFTS * (length + 1)]
    return tiled.reshape(resid.shape[:2] + (SHIFTS, length + 1))[..., :ticks]


def residual_of(prediction, measured, active):
    return (
        (prediction - measured.astype(jnp.float32)) * active.astype(jnp.float32)[..., None]
    ).astype(jnp.bfloat16)


def on_device(table, charge, hit_bins, hit_ticks, active, measured, row_module, col_module):
    tile_x, tile_y = (charge.shape[0], charge.shape[1])
    ticks = table.shape[2]
    parts_y = lax.axis_size("py")
    share = ticks // parts_y
    span = share + SHIFTS - 1
    weights = table.astype(jnp.bfloat16)
    row_start = px_index() * tile_x
    col_start = lax.axis_index("py") * tile_y

    deposits = jnp.stack(
        [charge, hit_bins.astype(jnp.float32), hit_ticks.astype(jnp.float32)], axis=-1
    )
    spread = jnp.broadcast_to(deposits[None], (parts_y,) + deposits.shape)
    band = jnp.transpose(lax.all_to_all(spread, "py", 0, 0), (1, 0, 2, 3, 4))
    band = band.reshape((tile_x, parts_y * tile_y) + deposits.shape[2:])
    above = passed_along(band[tile_x - 2 :], PX, 1)
    below = passed_along(band[:2], PX, -1)
    wide = jnp.concatenate([above, band, below], axis=0)
    binned = bin_charges(
        wide[..., 0], wide[..., 1].astype(jnp.int32), wide[..., 2].astype(jnp.int32)
    )
    source = jnp.pad(binned, ((0, 0), (2, 2), (0, 0), (0, 0)))
    width = source.shape[1] - 4
    rows_wide = lax.dynamic_slice_in_dim(
        jnp.pad(row_module, 2, constant_values=-1), row_start, tile_x + 4, 0
    )
    cols_all = jnp.pad(col_module, 2, constant_values=-1)

    stacked_band = gather_offsets(source, rows_wide, cols_all, tile_x, width)
    stacked = lax.dynamic_slice_in_dim(stacked_band, col_start, tile_y, 2)
    partial_value = jnp.einsum(
        "oxysb,obt->xyst", stacked, weights, preferred_element_type=jnp.float32
    )
    prediction = shift_sum(partial_value, ticks)
    resid = residual_of(prediction, measured, active)

    room = jnp.pad(resid, ((0, 0), (0, 0), (0, (parts_y + 1) * share - resid.shape[2])))
    lead = room[:, :, : parts_y * share].reshape(tile_x, tile_y, parts_y, share)
    rest = room[:, :, share : (parts_y + 1) * share].reshape(tile_x, tile_y, parts_y, share)
    sent = jnp.moveaxis(jnp.concatenate([lead, rest[..., : span - share]], axis=-1), 2, 0)
    got = lax.all_to_all(sent, "py", 0, 0)
    band_resid = jnp.transpose(got, (1, 0, 2, 3)).reshape(tile_x, width, span)

    gradient = jnp.einsum(
        "oxysb,xysu->obu",
        stacked_band,
        toeplitz(band_resid, share),
        preferred_element_type=jnp.float32,
    )
    flat = gradient.reshape(-1, share)
    summed = chip_sum(flat).reshape(gradient.shape)
    return (prediction.astype(jnp.bfloat16), summed / 16)


def solution(mesh):
    in_specs = (
        P(),
        P("px", "py", None),
        P("px", "py", None),
        P("px", "py", None),
        P("px", "py"),
        P("px", "py", None),
        P(),
        P(),
    )
    out_specs = (P("px", "py", None), P(None, None, "py"))
    rows_of = mesh.shape["px"]
    split = jax.sharding.Mesh(
        mesh.devices.reshape((rows_of // 2, 2) + mesh.devices.shape[1:]), ("pxa", "pxc", "py")
    )
    rename = lambda spec: P(*[PX if part == "px" else part for part in spec])
    return jax.shard_map(
        on_device,
        mesh=split,
        in_specs=tuple(rename(spec) for spec in in_specs),
        out_specs=tuple(rename(spec) for spec in out_specs),
        check_vma=False,
    )
```

```python
import jax
import jax.numpy as jnp
from jax import lax
from jax.sharding import PartitionSpec as P
from jax.experimental.layout import Layout, with_layout_constraint

BINS = 50
SHIFTS = 24
PX = ("pxa", "pxc")


def px_index():
    return lax.axis_index("pxa") * 2 + lax.axis_index("pxc")


def passed_along(block, axis, distance):
    devices = range(lax.axis_size("pxa") * 2)
    route = [(i - distance, i) for i in devices if i - distance in devices]
    return lax.ppermute(block, axis, route)


def tree_sum(value, axis):
    count = lax.axis_size(axis)
    me = lax.axis_index(axis)
    steps = count.bit_length() - 1
    rows = value.shape[0]
    unit = -(-rows // count)
    buf = jnp.pad(value, ((0, unit * count - rows),) + ((0, 0),) * (value.ndim - 1))
    bits = []
    for k in range(steps):
        gap = 1 << k
        bit = (me >> k) & 1
        bits.append(bit)
        half = buf.shape[0] // 2
        keep = lax.dynamic_slice_in_dim(buf, bit * half, half, 0)
        send = lax.dynamic_slice_in_dim(buf, (1 - bit) * half, half, 0)
        got = lax.ppermute(send, axis, [(p, p ^ gap) for p in range(count)])
        buf = keep + got
    for k in reversed(range(steps)):
        gap = 1 << k
        got = lax.ppermute(buf, axis, [(p, p ^ gap) for p in range(count)])
        low = jnp.where(bits[k] == 0, buf, got)
        high = jnp.where(bits[k] == 0, got, buf)
        buf = jnp.concatenate([low, high], axis=0)
    return buf[:rows]


def exchange_sum(value, axis):
    count = lax.axis_size(axis)
    rows = value.shape[0]
    unit = -(-rows // count)
    buf = jnp.pad(value, ((0, unit * count - rows),) + ((0, 0),) * (value.ndim - 1))
    pieces = buf.reshape((count, unit) + value.shape[1:])
    mine = jnp.sum(lax.all_to_all(pieces, axis, 0, 0), axis=0)
    spread = jnp.broadcast_to(mine[None], pieces.shape)
    every = lax.all_to_all(spread, axis, 0, 0)
    return every.reshape(buf.shape)[:rows]


def chip_sum(value):
    count = lax.axis_size("pxa")
    core = lax.axis_index("pxc")
    swap = [(0, 1), (1, 0)]
    rows = value.shape[0]
    unit = -(-rows // (2 * count))
    buf = jnp.pad(value, ((0, 2 * unit * count - rows),) + ((0, 0),) * (value.ndim - 1))
    half = unit * count
    keep = lax.dynamic_slice_in_dim(buf, core * half, half, 0)
    send = lax.dynamic_slice_in_dim(buf, (1 - core) * half, half, 0)
    part = keep + lax.ppermute(send, "pxc", swap)
    pieces = part.reshape((count, unit) + value.shape[1:]).astype(jnp.bfloat16)
    got = lax.all_to_all(pieces, "pxa", 0, 0).astype(jnp.float32)
    mine = jnp.sum(got, axis=0).astype(jnp.bfloat16)
    spread = jnp.broadcast_to(mine[None], pieces.shape)
    ours = lax.all_to_all(spread, "pxa", 0, 0).reshape((half,) + value.shape[1:])
    theirs = lax.ppermute(ours, "pxc", swap)
    low = jnp.where(core == 0, ours, theirs)
    high = jnp.where(core == 0, theirs, ours)
    return jnp.concatenate([low, high], axis=0)[:rows].astype(jnp.float32)


def bin_charges(charge, hit_bins, hit_ticks):
    tick_hot = (hit_ticks[..., None] == jnp.arange(SHIFTS, dtype=jnp.int32)).astype(jnp.float32)
    bin_hot = (hit_bins[..., None] == jnp.arange(BINS, dtype=jnp.int32)).astype(jnp.float32)
    weighted = charge[..., None] * tick_hot
    return jnp.einsum("xyks,xykb->xysb", weighted, bin_hot).astype(jnp.bfloat16)


def gather_offsets(source, rows, cols, count_x, count_y):
    pieces = []
    for row_off in range(-2, 3):
        for col_off in range(-2, 3):
            partial_value = source[
                2 - row_off : 2 - row_off + count_x, 2 - col_off : 2 - col_off + count_y
            ]
            row_same = rows[2 - row_off : 2 - row_off + count_x] == rows[2 : 2 + count_x]
            col_same = cols[2 - col_off : 2 - col_off + count_y] == cols[2 : 2 + count_y]
            allowed = row_same[:, None] & col_same[None, :]
            pieces.append(
                jnp.where(
                    allowed[:, :, None, None], partial_value, jnp.zeros((), partial_value.dtype)
                )
            )
    return jnp.stack(pieces, 0)


def shift_sum(partial_value, ticks):
    total = jnp.zeros(partial_value.shape[:2] + (ticks + SHIFTS,), jnp.float32)
    for offset in range(SHIFTS):
        total = total + jnp.pad(
            partial_value[:, :, offset, :], ((0, 0), (0, 0), (offset, SHIFTS - offset))
        )
    return total


def windows(resid, ticks):
    return jnp.stack([resid[:, :, offset : offset + ticks] for offset in range(SHIFTS)], axis=2)


def residual_of(prediction, measured, active):
    return (
        (prediction - measured.astype(jnp.float32)) * active.astype(jnp.float32)[..., None]
    ).astype(jnp.bfloat16)


def on_device(table, charge, hit_bins, hit_ticks, active, measured, row_module, col_module):
    tile_x, tile_y = (charge.shape[0], charge.shape[1])
    ticks = table.shape[2]
    parts_y = lax.axis_size("py")
    share = ticks // parts_y
    span = share + SHIFTS - 1
    weights = table.astype(jnp.bfloat16)
    row_start = px_index() * tile_x
    col_start = lax.axis_index("py") * tile_y

    deposits = jnp.stack(
        [charge, hit_bins.astype(jnp.float32), hit_ticks.astype(jnp.float32)], axis=-1
    )
    spread = jnp.broadcast_to(deposits[None], (parts_y,) + deposits.shape)
    band = jnp.transpose(lax.all_to_all(spread, "py", 0, 0), (1, 0, 2, 3, 4))
    band = band.reshape((tile_x, parts_y * tile_y) + deposits.shape[2:])
    above = passed_along(band[tile_x - 2 :], PX, 1)
    below = passed_along(band[:2], PX, -1)
    wide = jnp.concatenate([above, band, below], axis=0)
    binned = bin_charges(
        wide[..., 0], wide[..., 1].astype(jnp.int32), wide[..., 2].astype(jnp.int32)
    )
    source = jnp.pad(binned, ((0, 0), (2, 2), (0, 0), (0, 0)))
    width = source.shape[1] - 4
    rows_wide = lax.dynamic_slice_in_dim(
        jnp.pad(row_module, 2, constant_values=-1), row_start, tile_x + 4, 0
    )
    cols_all = jnp.pad(col_module, 2, constant_values=-1)

    stacked_band = with_layout_constraint(
        jnp.transpose(
            gather_offsets(source, rows_wide, cols_all, tile_x, width), (0, 1, 3, 2, 4)
        ),
        Layout(major_to_minor=(0, 1, 2, 3, 4)),
    )
    stacked = lax.dynamic_slice_in_dim(stacked_band, col_start, tile_y, 3)
    partial_value = jnp.einsum(
        "oxsyb,obt->xyst", stacked, weights, preferred_element_type=jnp.float32
    )
    prediction = shift_sum(partial_value, ticks)
    resid = residual_of(prediction, measured, active)

    room = jnp.pad(resid, ((0, 0), (0, 0), (0, (parts_y + 1) * share - resid.shape[2])))
    lead = room[:, :, : parts_y * share].reshape(tile_x, tile_y, parts_y, share)
    rest = room[:, :, share : (parts_y + 1) * share].reshape(tile_x, tile_y, parts_y, share)
    sent = jnp.moveaxis(jnp.concatenate([lead, rest[..., : span - share]], axis=-1), 2, 0)
    got = lax.all_to_all(sent, "py", 0, 0)
    band_resid = jnp.transpose(got, (1, 0, 2, 3)).reshape(tile_x, width, span)

    gradient = jnp.einsum(
        "oxsyb,xysu->obu",
        stacked_band,
        windows(band_resid, share),
        preferred_element_type=jnp.float32,
    )
    flat = gradient.reshape(-1, share)
    summed = chip_sum(flat).reshape(gradient.shape)
    return (prediction.astype(jnp.bfloat16), summed / 16)


def solution(mesh):
    in_specs = (
        P(),
        P("px", "py", None),
        P("px", "py", None),
        P("px", "py", None),
        P("px", "py"),
        P("px", "py", None),
        P(),
        P(),
    )
    out_specs = (P("px", "py", None), P(None, None, "py"))
    rows_of = mesh.shape["px"]
    split = jax.sharding.Mesh(
        mesh.devices.reshape((rows_of // 2, 2) + mesh.devices.shape[1:]), ("pxa", "pxc", "py")
    )
    rename = lambda spec: P(*[PX if part == "px" else part for part in spec])
    return jax.shard_map(
        on_device,
        mesh=split,
        in_specs=tuple(rename(spec) for spec in in_specs),
        out_specs=tuple(rename(spec) for spec in out_specs),
        check_vma=False,
    )
```

```python
import jax
import jax.numpy as jnp
from jax import lax
from jax.sharding import PartitionSpec as P

BINS = 50
SHIFTS = 24
PX = ("pxa", "pxc")


def px_index():
    return lax.axis_index("pxa") * 2 + lax.axis_index("pxc")


def passed_along(block, axis, distance):
    devices = range(lax.axis_size("pxa") * 2)
    route = [(i - distance, i) for i in devices if i - distance in devices]
    return lax.ppermute(block, axis, route)


def tree_sum(value, axis):
    count = lax.axis_size(axis)
    me = lax.axis_index(axis)
    steps = count.bit_length() - 1
    rows = value.shape[0]
    unit = -(-rows // count)
    buf = jnp.pad(value, ((0, unit * count - rows),) + ((0, 0),) * (value.ndim - 1))
    bits = []
    for k in range(steps):
        gap = 1 << k
        bit = (me >> k) & 1
        bits.append(bit)
        half = buf.shape[0] // 2
        keep = lax.dynamic_slice_in_dim(buf, bit * half, half, 0)
        send = lax.dynamic_slice_in_dim(buf, (1 - bit) * half, half, 0)
        got = lax.ppermute(send, axis, [(p, p ^ gap) for p in range(count)])
        buf = keep + got
    for k in reversed(range(steps)):
        gap = 1 << k
        got = lax.ppermute(buf, axis, [(p, p ^ gap) for p in range(count)])
        low = jnp.where(bits[k] == 0, buf, got)
        high = jnp.where(bits[k] == 0, got, buf)
        buf = jnp.concatenate([low, high], axis=0)
    return buf[:rows]


def exchange_sum(value, axis):
    count = lax.axis_size(axis)
    rows = value.shape[0]
    unit = -(-rows // count)
    buf = jnp.pad(value, ((0, unit * count - rows),) + ((0, 0),) * (value.ndim - 1))
    pieces = buf.reshape((count, unit) + value.shape[1:])
    mine = jnp.sum(lax.all_to_all(pieces, axis, 0, 0), axis=0)
    spread = jnp.broadcast_to(mine[None], pieces.shape)
    every = lax.all_to_all(spread, axis, 0, 0)
    return every.reshape(buf.shape)[:rows]


def chip_sum(value):
    count = lax.axis_size("pxa")
    core = lax.axis_index("pxc")
    swap = [(0, 1), (1, 0)]
    rows = value.shape[0]
    unit = -(-rows // (2 * count))
    buf = jnp.pad(value, ((0, 2 * unit * count - rows),) + ((0, 0),) * (value.ndim - 1))
    half = unit * count
    keep = lax.dynamic_slice_in_dim(buf, core * half, half, 0)
    send = lax.dynamic_slice_in_dim(buf, (1 - core) * half, half, 0)
    part = keep + lax.ppermute(send.astype(jnp.bfloat16), "pxc", swap).astype(jnp.float32)
    pieces = part.reshape((count, unit) + value.shape[1:]).astype(jnp.bfloat16)
    got = lax.all_to_all(pieces, "pxa", 0, 0).astype(jnp.float32)
    mine = jnp.sum(got, axis=0).astype(jnp.bfloat16)
    spread = jnp.broadcast_to(mine[None], pieces.shape)
    ours = lax.all_to_all(spread, "pxa", 0, 0).reshape((half,) + value.shape[1:])
    theirs = lax.ppermute(ours, "pxc", swap)
    low = jnp.where(core == 0, ours, theirs)
    high = jnp.where(core == 0, theirs, ours)
    return jnp.concatenate([low, high], axis=0)[:rows].astype(jnp.float32)


def bin_charges(charge, hit_bins, hit_ticks):
    tick_hot = (hit_ticks[..., None] == jnp.arange(SHIFTS, dtype=jnp.int32)).astype(jnp.float32)
    bin_hot = (hit_bins[..., None] == jnp.arange(BINS, dtype=jnp.int32)).astype(jnp.float32)
    weighted = charge[..., None] * tick_hot
    return jnp.einsum("xyks,xykb->xysb", weighted, bin_hot).astype(jnp.bfloat16)


def gather_offsets(source, rows, cols, count_x, count_y):
    pieces = []
    for row_off in range(-2, 3):
        for col_off in range(-2, 3):
            partial_value = source[
                2 - row_off : 2 - row_off + count_x, 2 - col_off : 2 - col_off + count_y
            ]
            row_same = rows[2 - row_off : 2 - row_off + count_x] == rows[2 : 2 + count_x]
            col_same = cols[2 - col_off : 2 - col_off + count_y] == cols[2 : 2 + count_y]
            allowed = row_same[:, None] & col_same[None, :]
            pieces.append(
                jnp.where(
                    allowed[:, :, None, None], partial_value, jnp.zeros((), partial_value.dtype)
                )
            )
    return jnp.stack(pieces, 0)


def shift_sum(partial_value, ticks):
    total = jnp.zeros(partial_value.shape[:2] + (ticks + SHIFTS,), jnp.float32)
    for offset in range(SHIFTS):
        total = total + jnp.pad(
            partial_value[:, :, offset, :], ((0, 0), (0, 0), (offset, SHIFTS - offset))
        )
    return total


def windows(resid, ticks):
    return jnp.stack([resid[:, :, offset : offset + ticks] for offset in range(SHIFTS)], axis=2)


def residual_of(prediction, measured, active):
    return (
        (prediction - measured.astype(jnp.float32)) * active.astype(jnp.float32)[..., None]
    ).astype(jnp.bfloat16)


def on_device(table, charge, hit_bins, hit_ticks, active, measured, row_module, col_module):
    tile_x, tile_y = (charge.shape[0], charge.shape[1])
    ticks = table.shape[2]
    parts_y = lax.axis_size("py")
    share = ticks // parts_y
    span = share + SHIFTS - 1
    weights = table.astype(jnp.bfloat16)
    row_start = px_index() * tile_x
    col_start = lax.axis_index("py") * tile_y

    deposits = jnp.stack(
        [charge, hit_bins.astype(jnp.float32), hit_ticks.astype(jnp.float32)], axis=-1
    )
    spread = jnp.broadcast_to(deposits[None], (parts_y,) + deposits.shape)
    band = jnp.transpose(lax.all_to_all(spread, "py", 0, 0), (1, 0, 2, 3, 4))
    band = band.reshape((tile_x, parts_y * tile_y) + deposits.shape[2:])
    above = passed_along(band[tile_x - 2 :], PX, 1)
    below = passed_along(band[:2], PX, -1)
    wide = jnp.concatenate([above, band, below], axis=0)
    binned = bin_charges(
        wide[..., 0], wide[..., 1].astype(jnp.int32), wide[..., 2].astype(jnp.int32)
    )
    source = jnp.pad(binned, ((0, 0), (2, 2), (0, 0), (0, 0)))
    width = source.shape[1] - 4
    rows_wide = lax.dynamic_slice_in_dim(
        jnp.pad(row_module, 2, constant_values=-1), row_start, tile_x + 4, 0
    )
    cols_all = jnp.pad(col_module, 2, constant_values=-1)

    stacked_band = gather_offsets(source, rows_wide, cols_all, tile_x, width)
    stacked = lax.dynamic_slice_in_dim(stacked_band, col_start, tile_y, 2)
    partial_value = jnp.einsum(
        "oxysb,obt->xyst", stacked, weights, preferred_element_type=jnp.float32
    )
    prediction = shift_sum(partial_value, ticks)
    resid = residual_of(prediction, measured, active)

    room = jnp.pad(resid, ((0, 0), (0, 0), (0, (parts_y + 1) * share - resid.shape[2])))
    lead = room[:, :, : parts_y * share].reshape(tile_x, tile_y, parts_y, share)
    rest = room[:, :, share : (parts_y + 1) * share].reshape(tile_x, tile_y, parts_y, share)
    sent = jnp.moveaxis(jnp.concatenate([lead, rest[..., : span - share]], axis=-1), 2, 0)
    got = lax.all_to_all(sent, "py", 0, 0)
    band_resid = jnp.transpose(got, (1, 0, 2, 3)).reshape(tile_x, width, span)

    gradient = jnp.einsum(
        "oxysb,xysu->obu",
        stacked_band,
        windows(band_resid, share),
        preferred_element_type=jnp.float32,
    )
    flat = gradient.reshape(-1, share)
    summed = chip_sum(flat).reshape(gradient.shape)
    return (prediction.astype(jnp.bfloat16), summed / 16)


def solution(mesh):
    in_specs = (
        P(),
        P("px", "py", None),
        P("px", "py", None),
        P("px", "py", None),
        P("px", "py"),
        P("px", "py", None),
        P(),
        P(),
    )
    out_specs = (P("px", "py", None), P(None, None, "py"))
    rows_of = mesh.shape["px"]
    split = jax.sharding.Mesh(
        mesh.devices.reshape((rows_of // 2, 2) + mesh.devices.shape[1:]), ("pxa", "pxc", "py")
    )
    rename = lambda spec: P(*[PX if part == "px" else part for part in spec])
    return jax.shard_map(
        on_device,
        mesh=split,
        in_specs=tuple(rename(spec) for spec in in_specs),
        out_specs=tuple(rename(spec) for spec in out_specs),
        check_vma=False,
    )
```

```python
import jax
import jax.numpy as jnp
from jax import lax
from jax.sharding import PartitionSpec as P

BINS = 50
SHIFTS = 24
PX = ("pxa", "pxc")


def px_index():
    return lax.axis_index("pxa") * 2 + lax.axis_index("pxc")


def passed_along(block, axis, distance):
    devices = range(lax.axis_size("pxa") * 2)
    route = [(i - distance, i) for i in devices if i - distance in devices]
    return lax.ppermute(block, axis, route)


def tree_sum(value, axis):
    count = lax.axis_size(axis)
    me = lax.axis_index(axis)
    steps = count.bit_length() - 1
    rows = value.shape[0]
    unit = -(-rows // count)
    buf = jnp.pad(value, ((0, unit * count - rows),) + ((0, 0),) * (value.ndim - 1))
    bits = []
    for k in range(steps):
        gap = 1 << k
        bit = (me >> k) & 1
        bits.append(bit)
        half = buf.shape[0] // 2
        keep = lax.dynamic_slice_in_dim(buf, bit * half, half, 0)
        send = lax.dynamic_slice_in_dim(buf, (1 - bit) * half, half, 0)
        got = lax.ppermute(send, axis, [(p, p ^ gap) for p in range(count)])
        buf = keep + got
    for k in reversed(range(steps)):
        gap = 1 << k
        got = lax.ppermute(buf, axis, [(p, p ^ gap) for p in range(count)])
        low = jnp.where(bits[k] == 0, buf, got)
        high = jnp.where(bits[k] == 0, got, buf)
        buf = jnp.concatenate([low, high], axis=0)
    return buf[:rows]


def exchange_sum(value, axis):
    count = lax.axis_size(axis)
    rows = value.shape[0]
    unit = -(-rows // count)
    buf = jnp.pad(value, ((0, unit * count - rows),) + ((0, 0),) * (value.ndim - 1))
    pieces = buf.reshape((count, unit) + value.shape[1:])
    mine = jnp.sum(lax.all_to_all(pieces, axis, 0, 0), axis=0)
    spread = jnp.broadcast_to(mine[None], pieces.shape)
    every = lax.all_to_all(spread, axis, 0, 0)
    return every.reshape(buf.shape)[:rows]


def chip_sum(value):
    count = lax.axis_size("pxa")
    core = lax.axis_index("pxc")
    swap = [(0, 1), (1, 0)]
    rows = value.shape[0]
    unit = -(-rows // (2 * count))
    buf = jnp.pad(value, ((0, 2 * unit * count - rows),) + ((0, 0),) * (value.ndim - 1))
    half = unit * count
    keep = lax.dynamic_slice_in_dim(buf, core * half, half, 0)
    send = lax.dynamic_slice_in_dim(buf, (1 - core) * half, half, 0)
    part = keep + lax.ppermute(send, "pxc", swap)
    pieces = part.reshape((count, unit) + value.shape[1:]).astype(jnp.bfloat16)
    got = lax.all_to_all(pieces, "pxa", 0, 0).astype(jnp.float32)
    mine = (jnp.sum(got, axis=0) * (1.0 / 16)).astype(jnp.bfloat16)
    spread = jnp.broadcast_to(mine[None], pieces.shape)
    ours = lax.all_to_all(spread, "pxa", 0, 0).reshape((half,) + value.shape[1:])
    theirs = lax.ppermute(ours, "pxc", swap)
    low = jnp.where(core == 0, ours, theirs)
    high = jnp.where(core == 0, theirs, ours)
    return jnp.concatenate([low, high], axis=0)[:rows].astype(jnp.float32)


def bin_charges(charge, hit_bins, hit_ticks):
    tick_hot = (hit_ticks[..., None] == jnp.arange(SHIFTS, dtype=jnp.int32)).astype(jnp.float32)
    bin_hot = (hit_bins[..., None] == jnp.arange(BINS, dtype=jnp.int32)).astype(jnp.float32)
    weighted = charge[..., None] * tick_hot
    return jnp.einsum("xyks,xykb->xysb", weighted, bin_hot).astype(jnp.bfloat16)


def gather_offsets(source, rows, cols, count_x, count_y):
    pieces = []
    for row_off in range(-2, 3):
        for col_off in range(-2, 3):
            partial_value = source[
                2 - row_off : 2 - row_off + count_x, 2 - col_off : 2 - col_off + count_y
            ]
            row_same = rows[2 - row_off : 2 - row_off + count_x] == rows[2 : 2 + count_x]
            col_same = cols[2 - col_off : 2 - col_off + count_y] == cols[2 : 2 + count_y]
            allowed = row_same[:, None] & col_same[None, :]
            pieces.append(
                jnp.where(
                    allowed[:, :, None, None], partial_value, jnp.zeros((), partial_value.dtype)
                )
            )
    return jnp.stack(pieces, 0)


def shift_sum(partial_value, ticks):
    total = jnp.zeros(partial_value.shape[:2] + (ticks + SHIFTS,), jnp.float32)
    for offset in range(SHIFTS):
        total = total + jnp.pad(
            partial_value[:, :, offset, :], ((0, 0), (0, 0), (offset, SHIFTS - offset))
        )
    return total


def windows(resid, ticks):
    return jnp.stack([resid[:, :, offset : offset + ticks] for offset in range(SHIFTS)], axis=2)


def residual_of(prediction, measured, active):
    return (
        (prediction - measured.astype(jnp.float32)) * active.astype(jnp.float32)[..., None]
    ).astype(jnp.bfloat16)


def on_device(table, charge, hit_bins, hit_ticks, active, measured, row_module, col_module):
    tile_x, tile_y = (charge.shape[0], charge.shape[1])
    ticks = table.shape[2]
    parts_y = lax.axis_size("py")
    share = ticks // parts_y
    span = share + SHIFTS - 1
    weights = table.astype(jnp.bfloat16)
    row_start = px_index() * tile_x
    col_start = lax.axis_index("py") * tile_y

    deposits = jnp.stack(
        [charge, hit_bins.astype(jnp.float32), hit_ticks.astype(jnp.float32)], axis=-1
    )
    spread = jnp.broadcast_to(deposits[None], (parts_y,) + deposits.shape)
    band = jnp.transpose(lax.all_to_all(spread, "py", 0, 0), (1, 0, 2, 3, 4))
    band = band.reshape((tile_x, parts_y * tile_y) + deposits.shape[2:])
    above = passed_along(band[tile_x - 2 :], PX, 1)
    below = passed_along(band[:2], PX, -1)
    wide = jnp.concatenate([above, band, below], axis=0)
    binned = bin_charges(
        wide[..., 0], wide[..., 1].astype(jnp.int32), wide[..., 2].astype(jnp.int32)
    )
    source = jnp.pad(binned, ((0, 0), (2, 2), (0, 0), (0, 0)))
    width = source.shape[1] - 4
    rows_wide = lax.dynamic_slice_in_dim(
        jnp.pad(row_module, 2, constant_values=-1), row_start, tile_x + 4, 0
    )
    cols_all = jnp.pad(col_module, 2, constant_values=-1)

    stacked_band = gather_offsets(source, rows_wide, cols_all, tile_x, width)
    stacked = lax.dynamic_slice_in_dim(stacked_band, col_start, tile_y, 2)
    partial_value = jnp.einsum(
        "oxysb,obt->xyst", stacked, weights, preferred_element_type=jnp.float32
    )
    prediction = shift_sum(partial_value, ticks)
    resid = residual_of(prediction, measured, active)

    room = jnp.pad(resid, ((0, 0), (0, 0), (0, (parts_y + 1) * share - resid.shape[2])))
    lead = room[:, :, : parts_y * share].reshape(tile_x, tile_y, parts_y, share)
    rest = room[:, :, share : (parts_y + 1) * share].reshape(tile_x, tile_y, parts_y, share)
    sent = jnp.moveaxis(jnp.concatenate([lead, rest[..., : span - share]], axis=-1), 2, 0)
    got = lax.all_to_all(sent, "py", 0, 0)
    band_resid = jnp.transpose(got, (1, 0, 2, 3)).reshape(tile_x, width, span)

    gradient = jnp.einsum(
        "oxysb,xysu->obu",
        stacked_band,
        windows(band_resid, share),
        preferred_element_type=jnp.float32,
    )
    flat = gradient.reshape(-1, share)
    summed = chip_sum(flat).reshape(gradient.shape)
    return (prediction.astype(jnp.bfloat16), summed)


def solution(mesh):
    in_specs = (
        P(),
        P("px", "py", None),
        P("px", "py", None),
        P("px", "py", None),
        P("px", "py"),
        P("px", "py", None),
        P(),
        P(),
    )
    out_specs = (P("px", "py", None), P(None, None, "py"))
    rows_of = mesh.shape["px"]
    split = jax.sharding.Mesh(
        mesh.devices.reshape((rows_of // 2, 2) + mesh.devices.shape[1:]), ("pxa", "pxc", "py")
    )
    rename = lambda spec: P(*[PX if part == "px" else part for part in spec])
    return jax.shard_map(
        on_device,
        mesh=split,
        in_specs=tuple(rename(spec) for spec in in_specs),
        out_specs=tuple(rename(spec) for spec in out_specs),
        check_vma=False,
    )
```
